512 devices in a mesh: freq: 16 (over y, core), sky: 32 (over z, x).
Axes of the slice: x: 4, y: 8, z: 8, core: 2. Of those that a mesh axis runs over, the one named last changes fastest.
Arguments:
- visibilities: bfloat16 [128, 2, 1024, 1024], P('freq', None, 'sky'), may hold values from -30 to 30
- templates: float32 [16, 128], replicated, may hold values from -0.5 to 0.5
Outputs:
- scores: float32 [16, 1024, 1024], P(None, 'freq', 'sky')
- continuum: float32 [9, 1024, 1024], P(None, 'freq', 'sky')
The draws below stay inside these ranges and needn't reach their ends.
All inputs are finite; a program needn't handle non-finite values.
Results may differ from the reference program's by a relative error of at most 0.006.
Values may be sent and summed in bfloat16 or wider, within the bound.
No kernel may reach another device: no remote copies, remote signals or barrier semaphores. Data moves between devices by JAX's collectives and lax.ppermute only.
A program may use at most 128 MiB of HBM per device.

```python
import jax
import jax.numpy as jnp
from jax import lax

GRID = 1024
ORDER = 8
TEMPLATES = 16
CHANNELS = 128


def draw_visibilities(key, part):
    key_noise = jax.random.fold_in(key, 11)
    key_rows = jax.random.fold_in(key, 23)
    shape = (CHANNELS, 2, GRID, GRID)
    chan_pos = jnp.arange(CHANNELS, dtype=jnp.float32) / jnp.float32(CHANNELS - 1)
    ramp = jnp.exp(jnp.log(3.0) * chan_pos)
    row_scale = jnp.exp(jax.random.uniform(key_rows, (CHANNELS, 1, GRID, 1), jnp.float32, 0.0, jnp.log(10.0))) / 4.0
    noise = jnp.clip(jax.random.normal(key_noise, shape, jnp.float32), -4.0, 4.0)
    return (noise * ramp[:, None, None, None] * row_scale).astype(jnp.bfloat16)


def bell_draw(rng, shape, scale, limit, held_as=jnp.bfloat16):
    entries = scale * jax.random.normal(rng, shape, jnp.float32)
    return jnp.clip(entries, min=-limit, max=limit).astype(held_as)


def setup_inputs(seed: int = 0) -> dict:
    key_of = jax.random.split(jax.random.key(seed), 3)
    visibilities = draw_visibilities(jax.random.fold_in(key_of[2], 71), 0)
    templates = bell_draw(key_of[1], (TEMPLATES, CHANNELS), CHANNELS ** -0.5, 0.5, jnp.float32)
    return dict(visibilities=visibilities, templates=templates)


epsilon = 1e-06

def tables(points):
    index = jnp.arange(points, dtype=jnp.int32)
    product = index[:, None] * index[None, :] % points
    angles = 2.0 * jnp.pi / points * product.astype(jnp.float32)
    factor = jnp.float32(points ** (-0.5))
    return ((jnp.cos(angles) * factor).astype(jnp.bfloat16), (jnp.sin(angles) * factor).astype(jnp.bfloat16))

def distances(row_pos, col_pos, points):
    half = jnp.float32(points / 2.0)
    row_term = (row_pos - half) * (row_pos - half)
    col_term = (col_pos - half) * (col_pos - half)
    return (row_term[:, None] + col_term[None, :]) / (half * half)

def filters(templates, channels, degree):
    abscissa = (2.0 * jnp.arange(channels, dtype=jnp.float32) - (channels - 1)) / jnp.float32(channels - 1)
    legendre = [jnp.ones((channels,), jnp.float32), abscissa]
    for order_idx in range(1, degree):
        legendre.append(((2 * order_idx + 1) * abscissa * legendre[order_idx] - order_idx * legendre[order_idx - 1]) / (order_idx + 1))
    legendre = legendre[:degree + 1]
    basis_rows = []
    for vector in legendre:
        for sweep in range(2):
            for earlier in basis_rows:
                vector = vector - jnp.sum(vector * earlier) * earlier
        vector = vector / jnp.sqrt(jnp.sum(vector * vector))
        basis_rows.append(vector)
    basis = jnp.stack(basis_rows)
    coeffs = jnp.dot(templates, basis.T, precision=lax.Precision.HIGHEST)
    matched = templates - jnp.dot(coeffs, basis, precision=lax.Precision.HIGHEST)
    return jnp.concatenate([matched, basis], axis=0).astype(jnp.bfloat16)

def reference(visibilities, templates):
    cosine, sine = tables(GRID)
    positions = jnp.arange(GRID, dtype=jnp.float32)
    dist = distances(positions, positions, GRID)

    def one_channel(item):
        grid_data, chan_index = item
        real_part, imag_part = (grid_data[0], grid_data[1])
        section_real = (jnp.dot(real_part, cosine, preferred_element_type=jnp.float32) - jnp.dot(imag_part, sine, preferred_element_type=jnp.float32)).astype(jnp.bfloat16)
        section_imag = (jnp.dot(real_part, sine, preferred_element_type=jnp.float32) + jnp.dot(imag_part, cosine, preferred_element_type=jnp.float32)).astype(jnp.bfloat16)
        picture = jnp.dot(cosine, section_real, preferred_element_type=jnp.float32) - jnp.dot(sine, section_imag, preferred_element_type=jnp.float32)
        stretch = 1.0 + 0.5 * chan_index.astype(jnp.float32) / jnp.float32(CHANNELS - 1)
        coef = -0.7 * stretch * stretch
        return (jnp.exp(coef * dist) * picture).astype(jnp.bfloat16)
    images = lax.map(one_channel, (visibilities, jnp.arange(CHANNELS, dtype=jnp.int32)))
    widened = images.astype(jnp.float32)
    power = jnp.sum(widened * widened)
    weights = filters(templates, CHANNELS, ORDER)
    projected = jnp.dot(weights, images.reshape(CHANNELS, GRID * GRID), preferred_element_type=jnp.float32)
    projected = projected.reshape(TEMPLATES + ORDER + 1, GRID, GRID)
    spread = jnp.sqrt(power / (CHANNELS * GRID * GRID) + epsilon)
    return (projected[:TEMPLATES] / spread, projected[TEMPLATES:])
```

```python
import numpy as np

import jax
import jax.numpy as jnp
from jax import lax
from jax.sharding import PartitionSpec as P

ORDER = 8


epsilon = 1e-06


def tables(points):
    block = 32
    index = jnp.arange(points, dtype=jnp.int32)
    step = jnp.arange(block, dtype=jnp.int32)
    factor = jnp.float32(points ** (-0.5))
    scale = jnp.float32(2.0 * np.pi / points)
    high = ((block * step)[:, None] * index[None, :]) % points
    low = (step[:, None] * index[None, :]) % points
    high_c = jnp.cos(scale * high.astype(jnp.float32))
    high_s = jnp.sin(scale * high.astype(jnp.float32))
    low_c = jnp.cos(scale * low.astype(jnp.float32))
    low_s = jnp.sin(scale * low.astype(jnp.float32))
    cos = high_c[:, None, :] * low_c[None, :, :] - high_s[:, None, :] * low_s[None, :, :]
    sin = high_s[:, None, :] * low_c[None, :, :] + high_c[:, None, :] * low_s[None, :, :]
    cos = (cos * factor).astype(jnp.bfloat16).reshape(points, points)
    sin = (sin * factor).astype(jnp.bfloat16).reshape(points, points)
    return lax.optimization_barrier((cos, sin))


def distances(row_pos, col_pos, points):
    half = jnp.float32(points / 2.0)
    row_term = (row_pos - half) * (row_pos - half)
    col_term = (col_pos - half) * (col_pos - half)
    return (row_term[:, None] + col_term[None, :]) / (half * half)


def basis_rows(channels, degree):
    abscissa = (2.0 * np.arange(channels, dtype=np.float64) - (channels - 1)) / (channels - 1)
    legendre = [np.ones((channels,), np.float64), abscissa]
    for order_idx in range(1, degree):
        legendre.append(
            (
                (2 * order_idx + 1) * abscissa * legendre[order_idx]
                - order_idx * legendre[order_idx - 1]
            )
            / (order_idx + 1)
        )
    legendre = legendre[: degree + 1]
    rows = []
    for vector in legendre:
        for sweep in range(2):
            for earlier in rows:
                vector = vector - np.sum(vector * earlier) * earlier
        vector = vector / np.sqrt(np.sum(vector * vector))
        rows.append(vector)
    return np.stack(rows).astype(np.float32)


def filters(templates, channels, degree):
    basis = jnp.asarray(basis_rows(channels, degree))
    coeffs = jnp.dot(templates, basis.T, precision=lax.Precision.HIGHEST)
    matched = templates - jnp.dot(coeffs, basis, precision=lax.Precision.HIGHEST)
    return jnp.concatenate([matched, basis], axis=0).astype(jnp.bfloat16)


def body(visibilities, templates):
    channels = visibilities.shape[0]
    row_count = visibilities.shape[2]
    points = visibilities.shape[3]
    num_templates = templates.shape[0]
    freq_count = lax.axis_size("freq")
    sky_count = lax.axis_size("sky")
    all_channels = channels * freq_count
    columns = points // sky_count
    lines = points // freq_count
    cosine, sine = tables(points)

    rows = visibilities.reshape(channels * 2 * row_count, points)
    with_cos = jnp.dot(rows, cosine, preferred_element_type=jnp.float32).reshape(
        channels, 2, row_count, points
    )
    with_sin = jnp.dot(rows, sine, preferred_element_type=jnp.float32).reshape(
        channels, 2, row_count, points
    )
    section_real = (with_cos[:, 0] - with_sin[:, 1]).astype(jnp.bfloat16)
    section_imag = (with_sin[:, 0] + with_cos[:, 1]).astype(jnp.bfloat16)
    stacked = jnp.stack([section_real, section_imag])
    stacked = stacked.reshape(2, channels, row_count, sky_count, columns)
    send = jnp.transpose(stacked, (3, 0, 2, 1, 4)).reshape(
        sky_count, 2, row_count, channels * columns
    )
    turned = lax.all_to_all(send, "sky", 0, 0, tiled=True)
    turned = turned.reshape(sky_count * 2 * row_count, channels * columns)

    table = jnp.stack(
        [
            cosine.reshape(points, sky_count, row_count),
            -sine.reshape(points, sky_count, row_count),
        ],
        axis=2,
    ).reshape(points, sky_count * 2 * row_count)
    picture = jnp.dot(table, turned, preferred_element_type=jnp.float32).reshape(
        points, channels, columns
    )
    row_pos = jnp.arange(points, dtype=jnp.float32)
    col_pos = (lax.axis_index("sky") * columns + jnp.arange(columns, dtype=jnp.int32)).astype(
        jnp.float32
    )
    chan_pos = (lax.axis_index("freq") * channels + jnp.arange(channels, dtype=jnp.int32)).astype(
        jnp.float32
    )
    stretch = 1.0 + 0.5 * chan_pos / jnp.float32(all_channels - 1)
    coef = -0.7 * stretch * stretch
    dist = distances(row_pos, col_pos, points)
    spectra = (jnp.exp(coef[None, :, None] * dist[:, None, :]) * picture).astype(jnp.bfloat16)
    widened = spectra.astype(jnp.float32)
    power_sum = lax.psum(jnp.sum(widened * widened), ("freq", "sky"))

    outgoing = jnp.transpose(
        spectra.reshape(freq_count, lines, channels, columns), (0, 2, 1, 3)
    )
    gathered = lax.all_to_all(outgoing, "freq", 0, 0, tiled=True)
    gathered = gathered.reshape(all_channels, lines * columns)
    weights = filters(templates, all_channels, ORDER)
    result = jnp.dot(weights, gathered, preferred_element_type=jnp.float32).reshape(
        weights.shape[0], lines, columns
    )
    spread = jnp.sqrt(power_sum / (all_channels * points * points) + epsilon)
    return (result[:num_templates] / spread, result[num_templates:])


def solution(mesh):
    return jax.shard_map(
        body,
        mesh=mesh,
        in_specs=(P("freq", None, "sky", None), P()),
        out_specs=(P(None, "freq", "sky"), P(None, "freq", "sky")),
        check_vma=False,
    )
```

```python
import numpy as np

import jax
import jax.numpy as jnp
from jax import lax
from jax.sharding import PartitionSpec as P

ORDER = 8


epsilon = 1e-06


def tables(points):
    block = 32
    index = jnp.arange(points, dtype=jnp.int32)
    step = jnp.arange(block, dtype=jnp.int32)
    factor = jnp.float32(points ** (-0.5))
    scale = jnp.float32(2.0 * np.pi / points)
    high = ((block * step)[:, None] * index[None, :]) % points
    low = (step[:, None] * index[None, :]) % points
    high_c = jnp.cos(scale * high.astype(jnp.float32))
    high_s = jnp.sin(scale * high.astype(jnp.float32))
    low_c = jnp.cos(scale * low.astype(jnp.float32))
    low_s = jnp.sin(scale * low.astype(jnp.float32))
    cos = high_c[:, None, :] * low_c[None, :, :] - high_s[:, None, :] * low_s[None, :, :]
    sin = high_s[:, None, :] * low_c[None, :, :] + high_c[:, None, :] * low_s[None, :, :]
    cos = (cos * factor).astype(jnp.bfloat16).reshape(points, points)
    sin = (sin * factor).astype(jnp.bfloat16).reshape(points, points)
    return lax.optimization_barrier((cos, sin))


def distances(row_pos, col_pos, points):
    half = jnp.float32(points / 2.0)
    row_term = (row_pos - half) * (row_pos - half)
    col_term = (col_pos - half) * (col_pos - half)
    return (row_term[:, None] + col_term[None, :]) / (half * half)


def basis_rows(channels, degree):
    abscissa = (2.0 * np.arange(channels, dtype=np.float64) - (channels - 1)) / (channels - 1)
    legendre = [np.ones((channels,), np.float64), abscissa]
    for order_idx in range(1, degree):
        legendre.append(
            (
                (2 * order_idx + 1) * abscissa * legendre[order_idx]
                - order_idx * legendre[order_idx - 1]
            )
            / (order_idx + 1)
        )
    legendre = legendre[: degree + 1]
    rows = []
    for vector in legendre:
        for sweep in range(2):
            for earlier in rows:
                vector = vector - np.sum(vector * earlier) * earlier
        vector = vector / np.sqrt(np.sum(vector * vector))
        rows.append(vector)
    return np.stack(rows).astype(np.float32)


def filters(templates, channels, degree):
    basis = jnp.asarray(basis_rows(channels, degree))
    coeffs = jnp.dot(templates, basis.T, precision=lax.Precision.HIGHEST)
    matched = templates - jnp.dot(coeffs, basis, precision=lax.Precision.HIGHEST)
    return jnp.concatenate([matched, basis], axis=0).astype(jnp.bfloat16)


def body(visibilities, templates):
    channels = visibilities.shape[0]
    row_count = visibilities.shape[2]
    points = visibilities.shape[3]
    num_templates = templates.shape[0]
    freq_count = lax.axis_size("freq")
    sky_count = lax.axis_size("sky")
    all_channels = channels * freq_count
    columns = points // sky_count
    lines = points // freq_count
    cosine, sine = tables(points)

    rows = visibilities.reshape(channels * 2 * row_count, points)
    with_cos = jnp.dot(rows, cosine, preferred_element_type=jnp.float32).reshape(
        channels, 2, row_count, points
    )
    with_sin = jnp.dot(rows, sine, preferred_element_type=jnp.float32).reshape(
        channels, 2, row_count, points
    )
    section_real = (with_cos[:, 0] - with_sin[:, 1]).astype(jnp.bfloat16)
    section_imag = (with_sin[:, 0] + with_cos[:, 1]).astype(jnp.bfloat16)
    stacked = jnp.stack([section_real, section_imag])
    stacked = stacked.reshape(2, channels, row_count, sky_count, columns)
    send = jnp.transpose(stacked, (3, 0, 2, 1, 4)).reshape(
        sky_count, 2, row_count, channels * columns
    )
    turned = lax.all_to_all(send, "sky", 0, 0, tiled=True)
    turned = turned.reshape(sky_count * 2 * row_count, channels * columns)

    table = jnp.stack(
        [
            cosine.reshape(points, sky_count, row_count),
            -sine.reshape(points, sky_count, row_count),
        ],
        axis=2,
    ).reshape(points, sky_count * 2 * row_count)
    picture = jnp.dot(table, turned, preferred_element_type=jnp.float32).reshape(
        points, channels, columns
    )
    row_pos = jnp.arange(points, dtype=jnp.float32)
    col_pos = (lax.axis_index("sky") * columns + jnp.arange(columns, dtype=jnp.int32)).astype(
        jnp.float32
    )
    chan_pos = (lax.axis_index("freq") * channels + jnp.arange(channels, dtype=jnp.int32)).astype(
        jnp.float32
    )
    stretch = 1.0 + 0.5 * chan_pos / jnp.float32(all_channels - 1)
    coef = -0.7 * stretch * stretch
    dist = distances(row_pos, col_pos, points)
    spectra = (jnp.exp(coef[None, :, None] * dist[:, None, :]) * picture).astype(jnp.bfloat16)
    widened = spectra.astype(jnp.float32)
    power_part = jnp.sum(widened * widened)

    outgoing = jnp.transpose(
        spectra.reshape(freq_count, lines, channels, columns), (0, 2, 1, 3)
    ).reshape(freq_count, channels * lines * columns)
    high = power_part.astype(jnp.bfloat16)
    rest = power_part - high.astype(jnp.float32)
    middle = rest.astype(jnp.bfloat16)
    low = (rest - middle.astype(jnp.float32)).astype(jnp.bfloat16)
    pieces = jnp.zeros((128,), jnp.bfloat16).at[0].set(high).at[1].set(middle).at[2].set(low)
    outgoing = jnp.concatenate(
        [outgoing, jnp.broadcast_to(pieces[None, :], (freq_count, 128))], axis=1
    )
    gathered = lax.all_to_all(outgoing, "freq", 0, 0, tiled=True)
    shares = gathered[:, channels * lines * columns :][:, :3].astype(jnp.float32)
    power_freq = jnp.sum(shares)
    images = gathered[:, : channels * lines * columns].reshape(all_channels, lines * columns)
    column_power = lax.all_to_all(
        jnp.broadcast_to(power_freq, (sky_count, 128)), "sky", 0, 0, tiled=True
    )
    power_sum = jnp.sum(column_power[:, 0])
    weights = filters(templates, all_channels, ORDER)
    result = jnp.dot(weights, images, preferred_element_type=jnp.float32).reshape(
        weights.shape[0], lines, columns
    )
    spread = jnp.sqrt(power_sum / (all_channels * points * points) + epsilon)
    return (result[:num_templates] / spread, result[num_templates:])


def solution(mesh):
    return jax.shard_map(
        body,
        mesh=mesh,
        in_specs=(P("freq", None, "sky", None), P()),
        out_specs=(P(None, "freq", "sky"), P(None, "freq", "sky")),
        check_vma=False,
    )
```

```python
import numpy as np

import jax
import jax.numpy as jnp
from jax import lax
from jax.sharding import PartitionSpec as P

ORDER = 8


epsilon = 1e-06


def tables(points, sources, depth):
    block = 32
    index = jnp.arange(points, dtype=jnp.int32)
    step = jnp.arange(block, dtype=jnp.int32)
    factor = jnp.float32(points ** (-0.5))
    scale = jnp.float32(2.0 * np.pi / points)
    high = ((block * step)[:, None] * index[None, :]) % points
    low = (step[:, None] * index[None, :]) % points
    high_c = jnp.cos(scale * high.astype(jnp.float32))
    high_s = jnp.sin(scale * high.astype(jnp.float32))
    low_c = jnp.cos(scale * low.astype(jnp.float32))
    low_s = jnp.sin(scale * low.astype(jnp.float32))
    cos = high_c[:, None, :] * low_c[None, :, :] - high_s[:, None, :] * low_s[None, :, :]
    sin = high_s[:, None, :] * low_c[None, :, :] + high_c[:, None, :] * low_s[None, :, :]
    cos = (cos * factor).astype(jnp.bfloat16).reshape(points, points)
    sin = (sin * factor).astype(jnp.bfloat16).reshape(points, points)

    def spread(x):
        x = x.reshape(block, sources, 1, depth)
        return jnp.concatenate([x, x], axis=2).reshape(block, sources * 2 * depth)

    part = (jnp.arange(sources * 2 * depth, dtype=jnp.int32) // depth) % 2 == 0
    hc, hs, lc, ls = spread(high_c), spread(high_s), spread(low_c), spread(low_s)
    first = jnp.where(part[None, :], hc, -hs)
    second = jnp.where(part[None, :], -hs, -hc)
    table = first[:, None, :] * lc[None, :, :] + second[:, None, :] * ls[None, :, :]
    table = (table * factor).astype(jnp.bfloat16).reshape(points, sources * 2 * depth)
    return lax.optimization_barrier((cos, sin)) + (lax.optimization_barrier(table),)


def distances(row_pos, col_pos, points):
    half = jnp.float32(points / 2.0)
    row_term = (row_pos - half) * (row_pos - half)
    col_term = (col_pos - half) * (col_pos - half)
    return (row_term[:, None] + col_term[None, :]) / (half * half)


def basis_rows(channels, degree):
    abscissa = (2.0 * np.arange(channels, dtype=np.float64) - (channels - 1)) / (channels - 1)
    legendre = [np.ones((channels,), np.float64), abscissa]
    for order_idx in range(1, degree):
        legendre.append(
            (
                (2 * order_idx + 1) * abscissa * legendre[order_idx]
                - order_idx * legendre[order_idx - 1]
            )
            / (order_idx + 1)
        )
    legendre = legendre[: degree + 1]
    rows = []
    for vector in legendre:
        for sweep in range(2):
            for earlier in rows:
                vector = vector - np.sum(vector * earlier) * earlier
        vector = vector / np.sqrt(np.sum(vector * vector))
        rows.append(vector)
    return np.stack(rows).astype(np.float32)


def filters(templates, channels, degree):
    basis = jnp.asarray(basis_rows(channels, degree))
    coeffs = jnp.dot(templates, basis.T, precision=lax.Precision.HIGHEST)
    matched = templates - jnp.dot(coeffs, basis, precision=lax.Precision.HIGHEST)
    return jnp.concatenate([matched, basis], axis=0).astype(jnp.bfloat16)


def body(visibilities, templates):
    channels = visibilities.shape[0]
    row_count = visibilities.shape[2]
    points = visibilities.shape[3]
    num_templates = templates.shape[0]
    freq_count = lax.axis_size("freq")
    sky_count = lax.axis_size("sky")
    all_channels = channels * freq_count
    columns = points // sky_count
    lines = points // freq_count
    cosine, sine, table = tables(points, sky_count, row_count)

    rows = visibilities.reshape(channels * 2 * row_count, points)
    with_cos = jnp.dot(rows, cosine, preferred_element_type=jnp.float32).reshape(
        channels, 2, row_count, points
    )
    with_sin = jnp.dot(rows, sine, preferred_element_type=jnp.float32).reshape(
        channels, 2, row_count, points
    )
    section_real = (with_cos[:, 0] - with_sin[:, 1]).astype(jnp.bfloat16)
    section_imag = (with_sin[:, 0] + with_cos[:, 1]).astype(jnp.bfloat16)
    stacked = jnp.stack([section_real, section_imag])
    stacked = stacked.reshape(2, channels, row_count, sky_count, columns)
    send = jnp.transpose(stacked, (3, 0, 2, 1, 4)).reshape(
        sky_count, 2, row_count, channels * columns
    )
    turned = lax.all_to_all(send, "sky", 0, 0, tiled=True)
    turned = turned.reshape(sky_count * 2 * row_count, channels * columns)

    picture = jnp.dot(table, turned, preferred_element_type=jnp.float32).reshape(
        points, channels, columns
    )
    row_pos = jnp.arange(points, dtype=jnp.float32)
    col_pos = (lax.axis_index("sky") * columns + jnp.arange(columns, dtype=jnp.int32)).astype(
        jnp.float32
    )
    chan_pos = (lax.axis_index("freq") * channels + jnp.arange(channels, dtype=jnp.int32)).astype(
        jnp.float32
    )
    stretch = 1.0 + 0.5 * chan_pos / jnp.float32(all_channels - 1)
    coef = -0.7 * stretch * stretch
    dist = distances(row_pos, col_pos, points)
    spectra = (jnp.exp(coef[None, :, None] * dist[:, None, :]) * picture).astype(jnp.bfloat16)
    widened = spectra.astype(jnp.float32)
    power_part = jnp.sum(widened * widened)

    high = power_part.astype(jnp.bfloat16)
    rest = power_part - high.astype(jnp.float32)
    middle = rest.astype(jnp.bfloat16)
    low = (rest - middle.astype(jnp.float32)).astype(jnp.bfloat16)
    pieces = jnp.zeros((channels * columns,), jnp.bfloat16)
    pieces = pieces.at[0].set(high).at[1].set(middle).at[2].set(low)
    outgoing = jnp.concatenate(
        [
            spectra.reshape(freq_count, lines, channels * columns),
            jnp.broadcast_to(pieces, (freq_count, 1, channels * columns)),
        ],
        axis=1,
    )
    gathered = lax.all_to_all(outgoing, "freq", 0, 0, tiled=True)
    power_freq = jnp.sum(gathered[:, lines, :3].astype(jnp.float32))
    column_power = lax.all_to_all(
        jnp.broadcast_to(power_freq, (sky_count, 128)), "sky", 0, 0, tiled=True
    )
    power_sum = jnp.sum(column_power[:, 0])
    images = gathered[:, :lines].reshape(freq_count, lines, channels, columns)
    weights = filters(templates, all_channels, ORDER).reshape(-1, freq_count, channels)
    result = jnp.einsum(
        "kfc,flcm->klm", weights, images, preferred_element_type=jnp.float32
    )
    spread = jnp.sqrt(power_sum / (all_channels * points * points) + epsilon)
    return (result[:num_templates] / spread, result[num_templates:])


def solution(mesh):
    return jax.shard_map(
        body,
        mesh=mesh,
        in_specs=(P("freq", None, "sky", None), P()),
        out_specs=(P(None, "freq", "sky"), P(None, "freq", "sky")),
        check_vma=False,
    )
```

```python
import numpy as np

import jax
import jax.numpy as jnp
from jax import lax
from jax.sharding import PartitionSpec as P

ORDER = 8


epsilon = 1e-06


def tables(points, sources, depth):
    block = 32
    index = jnp.arange(points, dtype=jnp.int32)
    step = jnp.arange(block, dtype=jnp.int32)
    factor = jnp.float32(points ** (-0.5))
    scale = jnp.float32(2.0 * np.pi / points)
    high = ((block * step)[:, None] * index[None, :]) % points
    low = (step[:, None] * index[None, :]) % points
    high_c = jnp.cos(scale * high.astype(jnp.float32))
    high_s = jnp.sin(scale * high.astype(jnp.float32))
    low_c = jnp.cos(scale * low.astype(jnp.float32))
    low_s = jnp.sin(scale * low.astype(jnp.float32))
    cos = high_c[:, None, :] * low_c[None, :, :] - high_s[:, None, :] * low_s[None, :, :]
    sin = high_s[:, None, :] * low_c[None, :, :] + high_c[:, None, :] * low_s[None, :, :]
    cos = (cos * factor).astype(jnp.bfloat16).reshape(points, points)
    sin = (sin * factor).astype(jnp.bfloat16).reshape(points, points)

    def spread(x):
        x = x.reshape(block, sources, 1, depth)
        return jnp.concatenate([x, x], axis=2).reshape(block, sources * 2 * depth)

    part = (jnp.arange(sources * 2 * depth, dtype=jnp.int32) // depth) % 2 == 0
    hc, hs, lc, ls = spread(high_c), spread(high_s), spread(low_c), spread(low_s)
    first = jnp.where(part[None, :], hc, -hs)
    second = jnp.where(part[None, :], -hs, -hc)
    table = first[:, None, :] * lc[None, :, :] + second[:, None, :] * ls[None, :, :]
    table = (table * factor).astype(jnp.bfloat16).reshape(points, sources * 2 * depth)
    return lax.optimization_barrier((cos, sin)) + (lax.optimization_barrier(table),)


def distances(row_pos, col_pos, points):
    half = jnp.float32(points / 2.0)
    row_term = (row_pos - half) * (row_pos - half)
    col_term = (col_pos - half) * (col_pos - half)
    return (row_term[:, None] + col_term[None, :]) / (half * half)


def basis_rows(channels, degree):
    abscissa = (2.0 * np.arange(channels, dtype=np.float64) - (channels - 1)) / (channels - 1)
    legendre = [np.ones((channels,), np.float64), abscissa]
    for order_idx in range(1, degree):
        legendre.append(
            (
                (2 * order_idx + 1) * abscissa * legendre[order_idx]
                - order_idx * legendre[order_idx - 1]
            )
            / (order_idx + 1)
        )
    legendre = legendre[: degree + 1]
    rows = []
    for vector in legendre:
        for sweep in range(2):
            for earlier in rows:
                vector = vector - np.sum(vector * earlier) * earlier
        vector = vector / np.sqrt(np.sum(vector * vector))
        rows.append(vector)
    return np.stack(rows).astype(np.float32)


def filters(templates, channels, degree):
    basis = jnp.asarray(basis_rows(channels, degree))
    coeffs = jnp.dot(templates, basis.T, precision=lax.Precision.HIGHEST)
    matched = templates - jnp.dot(coeffs, basis, precision=lax.Precision.HIGHEST)
    return jnp.concatenate([matched, basis], axis=0).astype(jnp.bfloat16)


def body(visibilities, templates):
    channels = visibilities.shape[0]
    row_count = visibilities.shape[2]
    points = visibilities.shape[3]
    num_templates = templates.shape[0]
    freq_count = lax.axis_size("freq")
    sky_count = lax.axis_size("sky")
    all_channels = channels * freq_count
    columns = points // sky_count
    lines = points // freq_count
    cosine, sine, table = tables(points, sky_count, row_count)

    with_cos = jnp.einsum(
        "vm,cpuv->mcpu", cosine, visibilities, preferred_element_type=jnp.float32
    )
    with_sin = jnp.einsum(
        "vm,cpuv->mcpu", sine, visibilities, preferred_element_type=jnp.float32
    )
    section_real = (with_cos[:, :, 0] - with_sin[:, :, 1]).astype(jnp.bfloat16)
    section_imag = (with_sin[:, :, 0] + with_cos[:, :, 1]).astype(jnp.bfloat16)
    stacked = jnp.stack([section_real, section_imag], axis=2)
    stacked = stacked.reshape(sky_count, columns, channels, 2, row_count)
    send = jnp.transpose(stacked, (0, 3, 4, 2, 1)).reshape(
        sky_count, 2, row_count, channels * columns
    )
    turned = lax.all_to_all(send, "sky", 0, 0, tiled=True)
    turned = turned.reshape(sky_count * 2 * row_count, channels * columns)

    picture = jnp.dot(table, turned, preferred_element_type=jnp.float32).reshape(
        points, channels, columns
    )
    row_pos = jnp.arange(points, dtype=jnp.float32)
    col_pos = (lax.axis_index("sky") * columns + jnp.arange(columns, dtype=jnp.int32)).astype(
        jnp.float32
    )
    chan_pos = (lax.axis_index("freq") * channels + jnp.arange(channels, dtype=jnp.int32)).astype(
        jnp.float32
    )
    stretch = 1.0 + 0.5 * chan_pos / jnp.float32(all_channels - 1)
    coef = -0.7 * stretch * stretch
    dist = distances(row_pos, col_pos, points)
    spectra = (jnp.exp(coef[None, :, None] * dist[:, None, :]) * picture).astype(jnp.bfloat16)
    widened = spectra.astype(jnp.float32)
    power_part = jnp.sum(widened * widened)

    high = power_part.astype(jnp.bfloat16)
    rest = power_part - high.astype(jnp.float32)
    middle = rest.astype(jnp.bfloat16)
    low = (rest - middle.astype(jnp.float32)).astype(jnp.bfloat16)
    pieces = jnp.zeros((channels * columns,), jnp.bfloat16)
    pieces = pieces.at[0].set(high).at[1].set(middle).at[2].set(low)
    outgoing = jnp.concatenate(
        [
            spectra.reshape(freq_count, lines, channels * columns),
            jnp.broadcast_to(pieces, (freq_count, 1, channels * columns)),
        ],
        axis=1,
    )
    gathered = lax.all_to_all(outgoing, "freq", 0, 0, tiled=True)
    power_freq = jnp.sum(gathered[:, lines, :3].astype(jnp.float32))
    column_power = lax.all_to_all(
        jnp.broadcast_to(power_freq, (sky_count, 128)), "sky", 0, 0, tiled=True
    )
    power_sum = jnp.sum(column_power[:, 0])
    images = gathered[:, :lines].reshape(freq_count, lines, channels, columns)
    weights = filters(templates, all_channels, ORDER).reshape(-1, freq_count, channels)
    result = jnp.einsum(
        "kfc,flcm->klm", weights, images, preferred_element_type=jnp.float32
    )
    spread = jnp.sqrt(power_sum / (all_channels * points * points) + epsilon)
    return (result[:num_templates] / spread, result[num_templates:])


def solution(mesh):
    return jax.shard_map(
        body,
        mesh=mesh,
        in_specs=(P("freq", None, "sky", None), P()),
        out_specs=(P(None, "freq", "sky"), P(None, "freq", "sky")),
        check_vma=False,
    )
```

```python
import numpy as np

import jax
import jax.numpy as jnp
from jax import lax
from jax.experimental import pallas as pl
from jax.experimental.pallas import tpu as pltpu
from jax.sharding import PartitionSpec as P

ORDER = 8


epsilon = 1e-06


def tables(points, sources, depth):
    block = 32
    index = jnp.arange(points, dtype=jnp.int32)
    step = jnp.arange(block, dtype=jnp.int32)
    factor = jnp.float32(points ** (-0.5))
    scale = jnp.float32(2.0 * np.pi / points)
    high = ((block * step)[:, None] * index[None, :]) % points
    low = (step[:, None] * index[None, :]) % points
    high_c = jnp.cos(scale * high.astype(jnp.float32))
    high_s = jnp.sin(scale * high.astype(jnp.float32))
    low_c = jnp.cos(scale * low.astype(jnp.float32))
    low_s = jnp.sin(scale * low.astype(jnp.float32))
    cos = high_c[:, None, :] * low_c[None, :, :] - high_s[:, None, :] * low_s[None, :, :]
    sin = high_s[:, None, :] * low_c[None, :, :] + high_c[:, None, :] * low_s[None, :, :]
    cos = (cos * factor).astype(jnp.bfloat16).reshape(points, points)
    sin = (sin * factor).astype(jnp.bfloat16).reshape(points, points)

    def spread(x):
        x = x.reshape(block, sources, 1, depth)
        return jnp.concatenate([x, x], axis=2).reshape(block, sources * 2 * depth)

    part = (jnp.arange(sources * 2 * depth, dtype=jnp.int32) // depth) % 2 == 0
    hc, hs, lc, ls = spread(high_c), spread(high_s), spread(low_c), spread(low_s)
    first = jnp.where(part[None, :], hc, -hs)
    second = jnp.where(part[None, :], -hs, -hc)
    table = first[:, None, :] * lc[None, :, :] + second[:, None, :] * ls[None, :, :]
    table = (table * factor).astype(jnp.bfloat16).reshape(points, sources * 2 * depth)
    return lax.optimization_barrier((cos, sin)) + (lax.optimization_barrier(table),)


def distances(row_pos, col_pos, points):
    half = jnp.float32(points / 2.0)
    row_term = (row_pos - half) * (row_pos - half)
    col_term = (col_pos - half) * (col_pos - half)
    return (row_term[:, None] + col_term[None, :]) / (half * half)


def basis_rows(channels, degree):
    abscissa = (2.0 * np.arange(channels, dtype=np.float64) - (channels - 1)) / (channels - 1)
    legendre = [np.ones((channels,), np.float64), abscissa]
    for order_idx in range(1, degree):
        legendre.append(
            (
                (2 * order_idx + 1) * abscissa * legendre[order_idx]
                - order_idx * legendre[order_idx - 1]
            )
            / (order_idx + 1)
        )
    legendre = legendre[: degree + 1]
    rows = []
    for vector in legendre:
        for sweep in range(2):
            for earlier in rows:
                vector = vector - np.sum(vector * earlier) * earlier
        vector = vector / np.sqrt(np.sum(vector * vector))
        rows.append(vector)
    return np.stack(rows).astype(np.float32)


def filters(templates, channels, degree):
    basis = jnp.asarray(basis_rows(channels, degree))
    coeffs = jnp.dot(templates, basis.T, precision=lax.Precision.HIGHEST)
    matched = templates - jnp.dot(coeffs, basis, precision=lax.Precision.HIGHEST)
    return jnp.concatenate([matched, basis], axis=0).astype(jnp.bfloat16)


def send_kernel(cos_ref, sin_ref, out_ref):
    channels = cos_ref.shape[0]
    lanes = cos_ref.shape[3]
    width = out_ref.shape[3] // channels
    per_vreg = lanes // width
    real = cos_ref[:, 0] - sin_ref[:, 1]
    imag = sin_ref[:, 0] + cos_ref[:, 1]
    lane_group = lax.broadcasted_iota(jnp.int32, real.shape[1:], 1) // width
    for q in range(out_ref.shape[0]):
        for p, part in enumerate((real, imag)):
            for h in range(channels // per_vreg):
                acc = jnp.zeros(part.shape[1:], jnp.float32)
                for j in range(per_vreg):
                    shift = (width * (j - q)) % lanes
                    piece = part[h * per_vreg + j]
                    if shift:
                        piece = pltpu.roll(piece, shift, 1)
                    acc = jnp.where(lane_group == j, piece, acc)
                out_ref[q, p, :, h * lanes:(h + 1) * lanes] = acc.astype(out_ref.dtype)


def make_send(with_cos, with_sin, sky_count, columns):
    channels, _, row_count, points = with_cos.shape
    lanes = 128
    per_step = lanes // columns
    spec_in = pl.BlockSpec((channels, 2, row_count, lanes), lambda t: (0, 0, 0, t))
    return pl.pallas_call(
        send_kernel,
        grid=(points // lanes,),
        in_specs=[spec_in, spec_in],
        out_specs=pl.BlockSpec(
            (per_step, 2, row_count, channels * columns), lambda t: (t, 0, 0, 0)
        ),
        out_shape=jax.ShapeDtypeStruct(
            (sky_count, 2, row_count, channels * columns), jnp.bfloat16
        ),
        cost_estimate=pl.CostEstimate(
            flops=2 * with_cos.size, transcendentals=0, bytes_accessed=5 * with_cos.size
        ),
    )(with_cos, with_sin)


def body(visibilities, templates):
    channels = visibilities.shape[0]
    row_count = visibilities.shape[2]
    points = visibilities.shape[3]
    num_templates = templates.shape[0]
    freq_count = lax.axis_size("freq")
    sky_count = lax.axis_size("sky")
    all_channels = channels * freq_count
    columns = points // sky_count
    lines = points // freq_count
    cosine, sine, table = tables(points, sky_count, row_count)

    rows = visibilities.reshape(channels * 2 * row_count, points)
    with_cos = jnp.dot(rows, cosine, preferred_element_type=jnp.float32).reshape(
        channels, 2, row_count, points
    )
    with_sin = jnp.dot(rows, sine, preferred_element_type=jnp.float32).reshape(
        channels, 2, row_count, points
    )
    send = make_send(with_cos, with_sin, sky_count, columns)
    turned = lax.all_to_all(send, "sky", 0, 0, tiled=True)
    turned = turned.reshape(sky_count * 2 * row_count, channels * columns)

    picture = jnp.dot(table, turned, preferred_element_type=jnp.float32).reshape(
        points, channels, columns
    )
    row_pos = jnp.arange(points, dtype=jnp.float32)
    col_pos = (lax.axis_index("sky") * columns + jnp.arange(columns, dtype=jnp.int32)).astype(
        jnp.float32
    )
    chan_pos = (lax.axis_index("freq") * channels + jnp.arange(channels, dtype=jnp.int32)).astype(
        jnp.float32
    )
    stretch = 1.0 + 0.5 * chan_pos / jnp.float32(all_channels - 1)
    coef = -0.7 * stretch * stretch
    dist = distances(row_pos, col_pos, points)
    spectra = (jnp.exp(coef[None, :, None] * dist[:, None, :]) * picture).astype(jnp.bfloat16)
    widened = spectra.astype(jnp.float32)
    power_part = jnp.sum(widened * widened)

    high = power_part.astype(jnp.bfloat16)
    rest = power_part - high.astype(jnp.float32)
    middle = rest.astype(jnp.bfloat16)
    low = (rest - middle.astype(jnp.float32)).astype(jnp.bfloat16)
    pieces = jnp.zeros((channels * columns,), jnp.bfloat16)
    pieces = pieces.at[0].set(high).at[1].set(middle).at[2].set(low)
    outgoing = jnp.concatenate(
        [
            spectra.reshape(freq_count, lines, channels * columns),
            jnp.broadcast_to(pieces, (freq_count, 1, channels * columns)),
        ],
        axis=1,
    )
    gathered = lax.all_to_all(outgoing, "freq", 0, 0, tiled=True)
    power_freq = jnp.sum(gathered[:, lines, :3].astype(jnp.float32))
    column_power = lax.all_to_all(
        jnp.broadcast_to(power_freq, (sky_count, 128)), "sky", 0, 0, tiled=True
    )
    power_sum = jnp.sum(column_power[:, 0])
    images = gathered[:, :lines].reshape(freq_count, lines, channels, columns)
    weights = filters(templates, all_channels, ORDER).reshape(-1, freq_count, channels)
    result = jnp.einsum(
        "kfc,flcm->klm", weights, images, preferred_element_type=jnp.float32
    )
    spread = jnp.sqrt(power_sum / (all_channels * points * points) + epsilon)
    return (result[:num_templates] / spread, result[num_templates:])


def solution(mesh):
    return jax.shard_map(
        body,
        mesh=mesh,
        in_specs=(P("freq", None, "sky", None), P()),
        out_specs=(P(None, "freq", "sky"), P(None, "freq", "sky")),
        check_vma=False,
    )
```

```python
import numpy as np

import jax
import jax.numpy as jnp
from jax import lax
from jax.experimental import pallas as pl
from jax.experimental.pallas import tpu as pltpu
from jax.sharding import PartitionSpec as P

ORDER = 8


epsilon = 1e-06


def tables(points, sources, depth):
    block = 32
    index = jnp.arange(points, dtype=jnp.int32)
    step = jnp.arange(block, dtype=jnp.int32)
    factor = jnp.float32(points ** (-0.5))
    scale = jnp.float32(2.0 * np.pi / points)
    high = ((block * step)[:, None] * index[None, :]) % points
    low = (step[:, None] * index[None, :]) % points
    high_c = jnp.cos(scale * high.astype(jnp.float32))
    high_s = jnp.sin(scale * high.astype(jnp.float32))
    low_c = jnp.cos(scale * low.astype(jnp.float32))
    low_s = jnp.sin(scale * low.astype(jnp.float32))
    cos = high_c[:, None, :] * low_c[None, :, :] - high_s[:, None, :] * low_s[None, :, :]
    sin = high_s[:, None, :] * low_c[None, :, :] + high_c[:, None, :] * low_s[None, :, :]
    cos = (cos * factor).astype(jnp.bfloat16).reshape(points, points)
    sin = (sin * factor).astype(jnp.bfloat16).reshape(points, points)

    def spread(x):
        x = x.reshape(block, sources, 1, depth)
        return jnp.concatenate([x, x], axis=2).reshape(block, sources * 2 * depth)

    part = (jnp.arange(sources * 2 * depth, dtype=jnp.int32) // depth) % 2 == 0
    hc, hs, lc, ls = spread(high_c), spread(high_s), spread(low_c), spread(low_s)
    first = jnp.where(part[None, :], hc, -hs)
    second = jnp.where(part[None, :], -hs, -hc)
    table = first[:, None, :] * lc[None, :, :] + second[:, None, :] * ls[None, :, :]
    table = (table * factor).astype(jnp.bfloat16).reshape(points, sources * 2 * depth)
    return lax.optimization_barrier((cos, sin)) + (lax.optimization_barrier(table),)


def distances(row_pos, col_pos, points):
    half = jnp.float32(points / 2.0)
    row_term = (row_pos - half) * (row_pos - half)
    col_term = (col_pos - half) * (col_pos - half)
    return (row_term[:, None] + col_term[None, :]) / (half * half)


def basis_rows(channels, degree):
    abscissa = (2.0 * np.arange(channels, dtype=np.float64) - (channels - 1)) / (channels - 1)
    legendre = [np.ones((channels,), np.float64), abscissa]
    for order_idx in range(1, degree):
        legendre.append(
            (
                (2 * order_idx + 1) * abscissa * legendre[order_idx]
                - order_idx * legendre[order_idx - 1]
            )
            / (order_idx + 1)
        )
    legendre = legendre[: degree + 1]
    rows = []
    for vector in legendre:
        for sweep in range(2):
            for earlier in rows:
                vector = vector - np.sum(vector * earlier) * earlier
        vector = vector / np.sqrt(np.sum(vector * vector))
        rows.append(vector)
    return np.stack(rows).astype(np.float32)


def filters(templates, channels, degree):
    basis = jnp.asarray(basis_rows(channels, degree))
    coeffs = jnp.dot(templates, basis.T, precision=lax.Precision.HIGHEST)
    matched = templates - jnp.dot(coeffs, basis, precision=lax.Precision.HIGHEST)
    return jnp.concatenate([matched, basis], axis=0).astype(jnp.bfloat16)


def send_kernel(cos_ref, sin_ref, out_ref):
    channels = cos_ref.shape[0]
    lanes = cos_ref.shape[3]
    width = out_ref.shape[3] // channels
    per_vreg = lanes // width
    real = cos_ref[:, 0] - sin_ref[:, 1]
    imag = sin_ref[:, 0] + cos_ref[:, 1]
    lane_group = lax.broadcasted_iota(jnp.int32, real.shape[1:], 1) // width
    for q in range(out_ref.shape[0]):
        for p, part in enumerate((real, imag)):
            for h in range(channels // per_vreg):
                acc = jnp.zeros(part.shape[1:], jnp.float32)
                for j in range(per_vreg):
                    shift = (width * (j - q)) % lanes
                    piece = part[h * per_vreg + j]
                    if shift:
                        piece = pltpu.roll(piece, shift, 1)
                    acc = jnp.where(lane_group == j, piece, acc)
                out_ref[q, p, :, h * lanes:(h + 1) * lanes] = acc.astype(out_ref.dtype)


def make_send(with_cos, with_sin, sky_count, columns):
    channels, _, row_count, points = with_cos.shape
    lanes = 128
    per_step = lanes // columns
    spec_in = pl.BlockSpec((channels, 2, row_count, lanes), lambda t: (0, 0, 0, t))
    return pl.pallas_call(
        send_kernel,
        grid=(points // lanes,),
        in_specs=[spec_in, spec_in],
        out_specs=pl.BlockSpec(
            (per_step, 2, row_count, channels * columns), lambda t: (t, 0, 0, 0)
        ),
        out_shape=jax.ShapeDtypeStruct(
            (sky_count, 2, row_count, channels * columns), jnp.bfloat16
        ),
        cost_estimate=pl.CostEstimate(
            flops=2 * with_cos.size, transcendentals=0, bytes_accessed=5 * with_cos.size
        ),
    )(with_cos, with_sin)


def body(visibilities, templates):
    channels = visibilities.shape[0]
    row_count = visibilities.shape[2]
    points = visibilities.shape[3]
    num_templates = templates.shape[0]
    freq_count = lax.axis_size("freq")
    sky_count = lax.axis_size("sky")
    all_channels = channels * freq_count
    columns = points // sky_count
    lines = points // freq_count
    cosine, sine, table = tables(points, sky_count, row_count)

    rows = visibilities.reshape(channels * 2 * row_count, points)
    with_cos = jnp.dot(rows, cosine, preferred_element_type=jnp.float32).reshape(
        channels, 2, row_count, points
    )
    with_sin = jnp.dot(rows, sine, preferred_element_type=jnp.float32).reshape(
        channels, 2, row_count, points
    )
    send = make_send(with_cos, with_sin, sky_count, columns)
    turned = lax.all_to_all(send, "sky", 0, 0, tiled=True)
    turned = turned.reshape(sky_count * 2 * row_count, channels * columns)

    picture = jnp.dot(table, turned, preferred_element_type=jnp.float32).reshape(
        points, channels, columns
    )
    row_pos = jnp.arange(points, dtype=jnp.float32)
    col_pos = (lax.axis_index("sky") * columns + jnp.arange(columns, dtype=jnp.int32)).astype(
        jnp.float32
    )
    chan_pos = (lax.axis_index("freq") * channels + jnp.arange(channels, dtype=jnp.int32)).astype(
        jnp.float32
    )
    stretch = 1.0 + 0.5 * chan_pos / jnp.float32(all_channels - 1)
    coef = -0.7 * stretch * stretch
    dist = distances(row_pos, col_pos, points)
    spectra = (jnp.exp(coef[None, :, None] * dist[:, None, :]) * picture).astype(jnp.bfloat16)
    widened = spectra.astype(jnp.float32)
    power_part = jnp.sum(widened * widened)

    totals = lax.psum_scatter(
        jnp.broadcast_to(power_part, (freq_count * sky_count, 128)),
        ("freq", "sky"), scatter_dimension=0, tiled=True,
    )
    power_sum = totals[0, 0]

    outgoing = spectra.reshape(freq_count, lines, channels * columns)
    gathered = lax.all_to_all(outgoing, "freq", 0, 0, tiled=True)
    images = gathered[:, :lines].reshape(freq_count, lines, channels, columns)
    weights = filters(templates, all_channels, ORDER).reshape(-1, freq_count, channels)
    result = jnp.einsum(
        "kfc,flcm->klm", weights, images, preferred_element_type=jnp.float32
    )
    spread = jnp.sqrt(power_sum / (all_channels * points * points) + epsilon)
    return (result[:num_templates] / spread, result[num_templates:])


def solution(mesh):
    return jax.shard_map(
        body,
        mesh=mesh,
        in_specs=(P("freq", None, "sky", None), P()),
        out_specs=(P(None, "freq", "sky"), P(None, "freq", "sky")),
        check_vma=False,
    )
```

```python
import numpy as np

import jax
import jax.numpy as jnp
from jax import lax
from jax.experimental import pallas as pl
from jax.experimental.pallas import tpu as pltpu
from jax.sharding import PartitionSpec as P

ORDER = 8


epsilon = 1e-06


def tables(points, sources, depth):
    block = 32
    index = jnp.arange(points, dtype=jnp.int32)
    step = jnp.arange(block, dtype=jnp.int32)
    factor = jnp.float32(points ** (-0.5))
    scale = jnp.float32(2.0 * np.pi / points)
    high = ((block * step)[:, None] * index[None, :]) % points
    low = (step[:, None] * index[None, :]) % points
    high_c = jnp.cos(scale * high.astype(jnp.float32))
    high_s = jnp.sin(scale * high.astype(jnp.float32))
    low_c = jnp.cos(scale * low.astype(jnp.float32))
    low_s = jnp.sin(scale * low.astype(jnp.float32))
    cos = high_c[:, None, :] * low_c[None, :, :] - high_s[:, None, :] * low_s[None, :, :]
    sin = high_s[:, None, :] * low_c[None, :, :] + high_c[:, None, :] * low_s[None, :, :]
    cos = (cos * factor).astype(jnp.bfloat16).reshape(points, points)
    sin = (sin * factor).astype(jnp.bfloat16).reshape(points, points)

    def spread(x):
        x = x.reshape(block, sources, 1, depth)
        return jnp.concatenate([x, x], axis=2).reshape(block, sources * 2 * depth)

    part = (jnp.arange(sources * 2 * depth, dtype=jnp.int32) // depth) % 2 == 0
    hc, hs, lc, ls = spread(high_c), spread(high_s), spread(low_c), spread(low_s)
    first = jnp.where(part[None, :], hc, -hs)
    second = jnp.where(part[None, :], -hs, -hc)
    table = first[:, None, :] * lc[None, :, :] + second[:, None, :] * ls[None, :, :]
    table = (table * factor).astype(jnp.bfloat16).reshape(points, sources * 2 * depth)
    return lax.optimization_barrier((cos, sin)) + (lax.optimization_barrier(table),)


def distances(row_pos, col_pos, points):
    half = jnp.float32(points / 2.0)
    row_term = (row_pos - half) * (row_pos - half)
    col_term = (col_pos - half) * (col_pos - half)
    return (row_term[:, None] + col_term[None, :]) / (half * half)


def basis_rows(channels, degree):
    abscissa = (2.0 * np.arange(channels, dtype=np.float64) - (channels - 1)) / (channels - 1)
    legendre = [np.ones((channels,), np.float64), abscissa]
    for order_idx in range(1, degree):
        legendre.append(
            (
                (2 * order_idx + 1) * abscissa * legendre[order_idx]
                - order_idx * legendre[order_idx - 1]
            )
            / (order_idx + 1)
        )
    legendre = legendre[: degree + 1]
    rows = []
    for vector in legendre:
        for sweep in range(2):
            for earlier in rows:
                vector = vector - np.sum(vector * earlier) * earlier
        vector = vector / np.sqrt(np.sum(vector * vector))
        rows.append(vector)
    return np.stack(rows).astype(np.float32)


def filters(templates, channels, degree):
    basis = jnp.asarray(basis_rows(channels, degree))
    coeffs = jnp.dot(templates, basis.T, precision=lax.Precision.HIGHEST)
    matched = templates - jnp.dot(coeffs, basis, precision=lax.Precision.HIGHEST)
    return jnp.concatenate([matched, basis], axis=0).astype(jnp.bfloat16)


def send_kernel(cos_ref, sin_ref, out_ref):
    channels = cos_ref.shape[0]
    lanes = cos_ref.shape[3]
    width = out_ref.shape[3] // channels
    per_vreg = lanes // width
    real = cos_ref[:, 0] - sin_ref[:, 1]
    imag = sin_ref[:, 0] + cos_ref[:, 1]
    lane_group = lax.broadcasted_iota(jnp.int32, real.shape[1:], 1) // width
    for q in range(out_ref.shape[0]):
        for p, part in enumerate((real, imag)):
            for h in range(channels // per_vreg):
                acc = jnp.zeros(part.shape[1:], jnp.float32)
                for j in range(per_vreg):
                    shift = (width * (j - q)) % lanes
                    piece = part[h * per_vreg + j]
                    if shift:
                        piece = pltpu.roll(piece, shift, 1)
                    acc = jnp.where(lane_group == j, piece, acc)
                out_ref[q, p, :, h * lanes:(h + 1) * lanes] = acc.astype(out_ref.dtype)


def make_send(with_cos, with_sin, sky_count, columns):
    channels, _, row_count, points = with_cos.shape
    lanes = 128
    per_step = lanes // columns
    spec_in = pl.BlockSpec((channels, 2, row_count, lanes), lambda t: (0, 0, 0, t))
    return pl.pallas_call(
        send_kernel,
        grid=(points // lanes,),
        in_specs=[spec_in, spec_in],
        out_specs=pl.BlockSpec(
            (per_step, 2, row_count, channels * columns), lambda t: (t, 0, 0, 0)
        ),
        out_shape=jax.ShapeDtypeStruct(
            (sky_count, 2, row_count, channels * columns), jnp.bfloat16
        ),
        cost_estimate=pl.CostEstimate(
            flops=2 * with_cos.size, transcendentals=0, bytes_accessed=5 * with_cos.size
        ),
    )(with_cos, with_sin)


def body(visibilities, templates):
    channels = visibilities.shape[0]
    row_count = visibilities.shape[2]
    points = visibilities.shape[3]
    num_templates = templates.shape[0]
    freq_count = lax.axis_size("freq")
    sky_count = lax.axis_size("sky")
    all_channels = channels * freq_count
    columns = points // sky_count
    lines = points // freq_count
    cosine, sine, table = tables(points, sky_count, row_count)

    rows = visibilities.reshape(channels * 2 * row_count, points)
    with_cos = jnp.dot(rows, cosine, preferred_element_type=jnp.float32).reshape(
        channels, 2, row_count, points
    )
    with_sin = jnp.dot(rows, sine, preferred_element_type=jnp.float32).reshape(
        channels, 2, row_count, points
    )
    send = make_send(with_cos, with_sin, sky_count, columns)
    turned = lax.all_to_all(send, "sky", 0, 0, tiled=True)
    turned = turned.reshape(sky_count * 2 * row_count, channels * columns)

    picture = jnp.dot(table, turned, preferred_element_type=jnp.float32).reshape(
        points, channels, columns
    )
    row_pos = jnp.arange(points, dtype=jnp.float32)
    col_pos = (lax.axis_index("sky") * columns + jnp.arange(columns, dtype=jnp.int32)).astype(
        jnp.float32
    )
    chan_pos = (lax.axis_index("freq") * channels + jnp.arange(channels, dtype=jnp.int32)).astype(
        jnp.float32
    )
    stretch = 1.0 + 0.5 * chan_pos / jnp.float32(all_channels - 1)
    coef = -0.7 * stretch * stretch
    dist = distances(row_pos, col_pos, points)
    spectra = (jnp.exp(coef[None, :, None] * dist[:, None, :]) * picture).astype(jnp.bfloat16)
    widened = spectra.astype(jnp.float32)
    power_part = jnp.sum(widened * widened)

    high = power_part.astype(jnp.bfloat16)
    rest = power_part - high.astype(jnp.float32)
    middle = rest.astype(jnp.bfloat16)
    low = (rest - middle.astype(jnp.float32)).astype(jnp.bfloat16)
    pieces = jnp.zeros((channels * columns,), jnp.bfloat16)
    pieces = pieces.at[0].set(high).at[1].set(middle).at[2].set(low)
    outgoing = jnp.concatenate(
        [
            spectra.reshape(freq_count, lines, channels * columns),
            jnp.broadcast_to(pieces, (freq_count, 1, channels * columns)),
        ],
        axis=1,
    )
    gathered = lax.all_to_all(outgoing, "freq", 0, 0, tiled=True)
    power_freq = jnp.sum(gathered[:, lines, :3].astype(jnp.float32))
    power_sum = jnp.broadcast_to(power_freq, (8, 128))
    distance = 1
    while distance < sky_count:
        pairs = [(i, i ^ distance) for i in range(sky_count)]
        power_sum = power_sum + lax.ppermute(power_sum, "sky", pairs)
        distance *= 2
    power_sum = power_sum[0, 0]
    images = gathered[:, :lines].reshape(freq_count, lines, channels, columns)
    weights = filters(templates, all_channels, ORDER).reshape(-1, freq_count, channels)
    result = jnp.einsum(
        "kfc,flcm->klm", weights, images, preferred_element_type=jnp.float32
    )
    spread = jnp.sqrt(power_sum / (all_channels * points * points) + epsilon)
    return (result[:num_templates] / spread, result[num_templates:])


def solution(mesh):
    return jax.shard_map(
        body,
        mesh=mesh,
        in_specs=(P("freq", None, "sky", None), P()),
        out_specs=(P(None, "freq", "sky"), P(None, "freq", "sky")),
        check_vma=False,
    )
```

```python
import numpy as np

import jax
import jax.numpy as jnp
from jax import lax
from jax.experimental import pallas as pl
from jax.experimental.pallas import tpu as pltpu
from jax.sharding import PartitionSpec as P

ORDER = 8


epsilon = 1e-06


def tables(points, sources, depth):
    block = 32
    index = jnp.arange(points, dtype=jnp.int32)
    step = jnp.arange(block, dtype=jnp.int32)
    factor = jnp.float32(points ** (-0.5))
    scale = jnp.float32(2.0 * np.pi / points)
    high = ((block * step)[:, None] * index[None, :]) % points
    low = (step[:, None] * index[None, :]) % points
    high_c = jnp.cos(scale * high.astype(jnp.float32))
    high_s = jnp.sin(scale * high.astype(jnp.float32))
    low_c = jnp.cos(scale * low.astype(jnp.float32))
    low_s = jnp.sin(scale * low.astype(jnp.float32))
    cos = high_c[:, None, :] * low_c[None, :, :] - high_s[:, None, :] * low_s[None, :, :]
    sin = high_s[:, None, :] * low_c[None, :, :] + high_c[:, None, :] * low_s[None, :, :]
    cos = (cos * factor).astype(jnp.bfloat16).reshape(points, points)
    sin = (sin * factor).astype(jnp.bfloat16).reshape(points, points)

    def spread(x):
        x = x.reshape(block, sources, 1, depth)
        return jnp.concatenate([x, x], axis=2).reshape(block, sources * 2 * depth)

    part = (jnp.arange(sources * 2 * depth, dtype=jnp.int32) // depth) % 2 == 0
    hc, hs, lc, ls = spread(high_c), spread(high_s), spread(low_c), spread(low_s)
    first = jnp.where(part[None, :], hc, -hs)
    second = jnp.where(part[None, :], -hs, -hc)
    table = first[:, None, :] * lc[None, :, :] + second[:, None, :] * ls[None, :, :]
    table = (table * factor).astype(jnp.bfloat16).reshape(points, sources * 2 * depth)
    return lax.optimization_barrier((cos, sin)) + (lax.optimization_barrier(table),)


def distances(row_pos, col_pos, points):
    half = jnp.float32(points / 2.0)
    row_term = (row_pos - half) * (row_pos - half)
    col_term = (col_pos - half) * (col_pos - half)
    return (row_term[:, None] + col_term[None, :]) / (half * half)


def basis_rows(channels, degree):
    abscissa = (2.0 * np.arange(channels, dtype=np.float64) - (channels - 1)) / (channels - 1)
    legendre = [np.ones((channels,), np.float64), abscissa]
    for order_idx in range(1, degree):
        legendre.append(
            (
                (2 * order_idx + 1) * abscissa * legendre[order_idx]
                - order_idx * legendre[order_idx - 1]
            )
            / (order_idx + 1)
        )
    legendre = legendre[: degree + 1]
    rows = []
    for vector in legendre:
        for sweep in range(2):
            for earlier in rows:
                vector = vector - np.sum(vector * earlier) * earlier
        vector = vector / np.sqrt(np.sum(vector * vector))
        rows.append(vector)
    return np.stack(rows).astype(np.float32)


def filters(templates, channels, degree):
    basis = jnp.asarray(basis_rows(channels, degree))
    coeffs = jnp.dot(templates, basis.T, precision=lax.Precision.HIGHEST)
    matched = templates - jnp.dot(coeffs, basis, precision=lax.Precision.HIGHEST)
    return jnp.concatenate([matched, basis], axis=0).astype(jnp.bfloat16)


def send_kernel(cos_ref, sin_ref, out_ref):
    channels = cos_ref.shape[0]
    lanes = cos_ref.shape[3]
    width = out_ref.shape[3] // channels
    per_vreg = lanes // width
    real = (cos_ref[:, 0] - sin_ref[:, 1]).astype(out_ref.dtype)
    imag = (sin_ref[:, 0] + cos_ref[:, 1]).astype(out_ref.dtype)
    lane_group = lax.broadcasted_iota(jnp.int32, real.shape[1:], 1) // width
    for q in range(out_ref.shape[0]):
        for p, part in enumerate((real, imag)):
            for h in range(channels // per_vreg):
                acc = jnp.zeros(part.shape[1:], part.dtype)
                for j in range(per_vreg):
                    shift = (width * (j - q)) % lanes
                    piece = part[h * per_vreg + j]
                    if shift:
                        piece = pltpu.roll(piece, shift, 1)
                    acc = jnp.where(lane_group == j, piece, acc)
                out_ref[q, p, :, h * lanes:(h + 1) * lanes] = acc


def make_send(with_cos, with_sin, sky_count, columns):
    channels, _, row_count, points = with_cos.shape
    lanes = 128
    per_step = lanes // columns
    spec_in = pl.BlockSpec((channels, 2, row_count, lanes), lambda t: (0, 0, 0, t))
    return pl.pallas_call(
        send_kernel,
        grid=(points // lanes,),
        in_specs=[spec_in, spec_in],
        out_specs=pl.BlockSpec(
            (per_step, 2, row_count, channels * columns), lambda t: (t, 0, 0, 0)
        ),
        out_shape=jax.ShapeDtypeStruct(
            (sky_count, 2, row_count, channels * columns), jnp.bfloat16
        ),
        cost_estimate=pl.CostEstimate(
            flops=2 * with_cos.size, transcendentals=0, bytes_accessed=5 * with_cos.size
        ),
    )(with_cos, with_sin)


def body(visibilities, templates):
    channels = visibilities.shape[0]
    row_count = visibilities.shape[2]
    points = visibilities.shape[3]
    num_templates = templates.shape[0]
    freq_count = lax.axis_size("freq")
    sky_count = lax.axis_size("sky")
    all_channels = channels * freq_count
    columns = points // sky_count
    lines = points // freq_count
    cosine, sine, table = tables(points, sky_count, row_count)

    rows = visibilities.reshape(channels * 2 * row_count, points)
    with_cos = jnp.dot(rows, cosine, preferred_element_type=jnp.float32).reshape(
        channels, 2, row_count, points
    )
    with_sin = jnp.dot(rows, sine, preferred_element_type=jnp.float32).reshape(
        channels, 2, row_count, points
    )
    send = make_send(with_cos, with_sin, sky_count, columns)
    turned = lax.all_to_all(send, "sky", 0, 0, tiled=True)
    turned = turned.reshape(sky_count * 2 * row_count, channels * columns)

    picture = jnp.dot(table, turned, preferred_element_type=jnp.float32).reshape(
        points, channels, columns
    )
    row_pos = jnp.arange(points, dtype=jnp.float32)
    col_pos = (lax.axis_index("sky") * columns + jnp.arange(columns, dtype=jnp.int32)).astype(
        jnp.float32
    )
    chan_pos = (lax.axis_index("freq") * channels + jnp.arange(channels, dtype=jnp.int32)).astype(
        jnp.float32
    )
    stretch = 1.0 + 0.5 * chan_pos / jnp.float32(all_channels - 1)
    coef = -0.7 * stretch * stretch
    dist = distances(row_pos, col_pos, points)
    spectra = (jnp.exp(coef[None, :, None] * dist[:, None, :]) * picture).astype(jnp.bfloat16)
    widened = spectra.astype(jnp.float32)
    power_part = jnp.sum(widened * widened)

    high = power_part.astype(jnp.bfloat16)
    rest = power_part - high.astype(jnp.float32)
    middle = rest.astype(jnp.bfloat16)
    low = (rest - middle.astype(jnp.float32)).astype(jnp.bfloat16)
    pieces = jnp.zeros((channels * columns,), jnp.bfloat16)
    pieces = pieces.at[0].set(high).at[1].set(middle).at[2].set(low)
    outgoing = jnp.concatenate(
        [
            spectra.reshape(freq_count, lines, channels * columns),
            jnp.broadcast_to(pieces, (freq_count, 1, channels * columns)),
        ],
        axis=1,
    )
    gathered = lax.all_to_all(outgoing, "freq", 0, 0, tiled=True)
    power_freq = jnp.sum(gathered[:, lines, :3].astype(jnp.float32))
    column_power = lax.all_to_all(
        jnp.broadcast_to(power_freq, (sky_count, 128)), "sky", 0, 0, tiled=True
    )
    power_sum = jnp.sum(column_power[:, 0])
    images = gathered[:, :lines].reshape(freq_count, lines, channels, columns)
    weights = filters(templates, all_channels, ORDER).reshape(-1, freq_count, channels)
    result = jnp.einsum(
        "kfc,flcm->klm", weights, images, preferred_element_type=jnp.float32
    )
    spread = jnp.sqrt(power_sum / (all_channels * points * points) + epsilon)
    return (result[:num_templates] / spread, result[num_templates:])


def solution(mesh):
    return jax.shard_map(
        body,
        mesh=mesh,
        in_specs=(P("freq", None, "sky", None), P()),
        out_specs=(P(None, "freq", "sky"), P(None, "freq", "sky")),
        check_vma=False,
    )
```

```python
import numpy as np

import jax
import jax.numpy as jnp
from jax import lax
from jax.experimental import pallas as pl
from jax.experimental.pallas import tpu as pltpu
from jax.sharding import PartitionSpec as P

ORDER = 8


epsilon = 1e-06


def tables(points, sources, depth):
    block = 32
    index = jnp.arange(points, dtype=jnp.int32)
    step = jnp.arange(block, dtype=jnp.int32)
    factor = jnp.float32(points ** (-0.5))
    scale = jnp.float32(2.0 * np.pi / points)
    high = ((block * step)[:, None] * index[None, :]) % points
    low = (step[:, None] * index[None, :]) % points
    high_c = jnp.cos(scale * high.astype(jnp.float32))
    high_s = jnp.sin(scale * high.astype(jnp.float32))
    low_c = jnp.cos(scale * low.astype(jnp.float32))
    low_s = jnp.sin(scale * low.astype(jnp.float32))
    cos = high_c[:, None, :] * low_c[None, :, :] - high_s[:, None, :] * low_s[None, :, :]
    sin = high_s[:, None, :] * low_c[None, :, :] + high_c[:, None, :] * low_s[None, :, :]
    cos = (cos * factor).astype(jnp.bfloat16).reshape(points, points)
    sin = (sin * factor).astype(jnp.bfloat16).reshape(points, points)

    def spread(x):
        x = x.reshape(block, sources, 1, depth)
        return jnp.concatenate([x, x], axis=2).reshape(block, sources * 2 * depth)

    part = (jnp.arange(sources * 2 * depth, dtype=jnp.int32) // depth) % 2 == 0
    hc, hs, lc, ls = spread(high_c), spread(high_s), spread(low_c), spread(low_s)
    first = jnp.where(part[None, :], hc, -hs)
    second = jnp.where(part[None, :], -hs, -hc)
    table = first[:, None, :] * lc[None, :, :] + second[:, None, :] * ls[None, :, :]
    table = (table * factor).astype(jnp.bfloat16).reshape(points, sources * 2 * depth)
    return lax.optimization_barrier((cos, sin)) + (lax.optimization_barrier(table),)


def distances(row_pos, col_pos, points):
    half = jnp.float32(points / 2.0)
    row_term = (row_pos - half) * (row_pos - half)
    col_term = (col_pos - half) * (col_pos - half)
    return (row_term[:, None] + col_term[None, :]) / (half * half)


def basis_rows(channels, degree):
    abscissa = (2.0 * np.arange(channels, dtype=np.float64) - (channels - 1)) / (channels - 1)
    legendre = [np.ones((channels,), np.float64), abscissa]
    for order_idx in range(1, degree):
        legendre.append(
            (
                (2 * order_idx + 1) * abscissa * legendre[order_idx]
                - order_idx * legendre[order_idx - 1]
            )
            / (order_idx + 1)
        )
    legendre = legendre[: degree + 1]
    rows = []
    for vector in legendre:
        for sweep in range(2):
            for earlier in rows:
                vector = vector - np.sum(vector * earlier) * earlier
        vector = vector / np.sqrt(np.sum(vector * vector))
        rows.append(vector)
    return np.stack(rows).astype(np.float32)


def filters(templates, channels, degree):
    basis = jnp.asarray(basis_rows(channels, degree))
    coeffs = jnp.dot(templates, basis.T, precision=lax.Precision.HIGHEST)
    matched = templates - jnp.dot(coeffs, basis, precision=lax.Precision.HIGHEST)
    return jnp.concatenate([matched, basis], axis=0).astype(jnp.bfloat16)


def send_kernel(cos_ref, sin_ref, out_ref):
    channels = cos_ref.shape[0]
    points = cos_ref.shape[3]
    lanes = 128
    width = out_ref.shape[3] // channels
    per_vreg = lanes // width
    real = cos_ref[:, 0] - sin_ref[:, 1]
    imag = sin_ref[:, 0] + cos_ref[:, 1]
    lane_group = lax.broadcasted_iota(jnp.int32, (real.shape[1], lanes), 1) // width
    for t in range(points // lanes):
        for p, part in enumerate((real, imag)):
            block = part[:, :, t * lanes:(t + 1) * lanes]
            for q in range(per_vreg):
                for h in range(channels // per_vreg):
                    acc = jnp.zeros(block.shape[1:], jnp.float32)
                    for j in range(per_vreg):
                        shift = (width * (j - q)) % lanes
                        piece = block[h * per_vreg + j]
                        if shift:
                            piece = pltpu.roll(piece, shift, 1)
                        acc = jnp.where(lane_group == j, piece, acc)
                    out_ref[t * per_vreg + q, p, :, h * lanes:(h + 1) * lanes] = acc.astype(
                        out_ref.dtype
                    )


def make_send(with_cos, with_sin, sky_count, columns):
    channels, _, row_count, points = with_cos.shape
    rows = 8
    spec_in = pl.BlockSpec((channels, 2, rows, points), lambda r: (0, 0, r, 0))
    return pl.pallas_call(
        send_kernel,
        grid=(row_count // rows,),
        in_specs=[spec_in, spec_in],
        out_specs=pl.BlockSpec(
            (sky_count, 2, rows, channels * columns), lambda r: (0, 0, r, 0)
        ),
        out_shape=jax.ShapeDtypeStruct(
            (sky_count, 2, row_count, channels * columns), jnp.bfloat16
        ),
        cost_estimate=pl.CostEstimate(
            flops=2 * with_cos.size, transcendentals=0, bytes_accessed=5 * with_cos.size
        ),
    )(with_cos, with_sin)


def body(visibilities, templates):
    channels = visibilities.shape[0]
    row_count = visibilities.shape[2]
    points = visibilities.shape[3]
    num_templates = templates.shape[0]
    freq_count = lax.axis_size("freq")
    sky_count = lax.axis_size("sky")
    all_channels = channels * freq_count
    columns = points // sky_count
    lines = points // freq_count
    cosine, sine, table = tables(points, sky_count, row_count)

    rows = visibilities.reshape(channels * 2 * row_count, points)
    with_cos = jnp.dot(rows, cosine, preferred_element_type=jnp.float32).reshape(
        channels, 2, row_count, points
    )
    with_sin = jnp.dot(rows, sine, preferred_element_type=jnp.float32).reshape(
        channels, 2, row_count, points
    )
    send = make_send(with_cos, with_sin, sky_count, columns)
    turned = lax.all_to_all(send, "sky", 0, 0, tiled=True)
    turned = turned.reshape(sky_count * 2 * row_count, channels * columns)

    picture = jnp.dot(table, turned, preferred_element_type=jnp.float32).reshape(
        points, channels, columns
    )
    row_pos = jnp.arange(points, dtype=jnp.float32)
    col_pos = (lax.axis_index("sky") * columns + jnp.arange(columns, dtype=jnp.int32)).astype(
        jnp.float32
    )
    chan_pos = (lax.axis_index("freq") * channels + jnp.arange(channels, dtype=jnp.int32)).astype(
        jnp.float32
    )
    stretch = 1.0 + 0.5 * chan_pos / jnp.float32(all_channels - 1)
    coef = -0.7 * stretch * stretch
    dist = distances(row_pos, col_pos, points)
    spectra = (jnp.exp(coef[None, :, None] * dist[:, None, :]) * picture).astype(jnp.bfloat16)
    widened = spectra.astype(jnp.float32)
    power_part = jnp.sum(widened * widened)

    high = power_part.astype(jnp.bfloat16)
    rest = power_part - high.astype(jnp.float32)
    middle = rest.astype(jnp.bfloat16)
    low = (rest - middle.astype(jnp.float32)).astype(jnp.bfloat16)
    pieces = jnp.zeros((channels * columns,), jnp.bfloat16)
    pieces = pieces.at[0].set(high).at[1].set(middle).at[2].set(low)
    outgoing = jnp.concatenate(
        [
            spectra.reshape(freq_count, lines, channels * columns),
            jnp.broadcast_to(pieces, (freq_count, 1, channels * columns)),
        ],
        axis=1,
    )
    gathered = lax.all_to_all(outgoing, "freq", 0, 0, tiled=True)
    power_freq = jnp.sum(gathered[:, lines, :3].astype(jnp.float32))
    column_power = lax.all_to_all(
        jnp.broadcast_to(power_freq, (sky_count, 128)), "sky", 0, 0, tiled=True
    )
    power_sum = jnp.sum(column_power[:, 0])
    images = gathered[:, :lines].reshape(freq_count, lines, channels, columns)
    weights = filters(templates, all_channels, ORDER).reshape(-1, freq_count, channels)
    result = jnp.einsum(
        "kfc,flcm->klm", weights, images, preferred_element_type=jnp.float32
    )
    spread = jnp.sqrt(power_sum / (all_channels * points * points) + epsilon)
    return (result[:num_templates] / spread, result[num_templates:])


def solution(mesh):
    return jax.shard_map(
        body,
        mesh=mesh,
        in_specs=(P("freq", None, "sky", None), P()),
        out_specs=(P(None, "freq", "sky"), P(None, "freq", "sky")),
        check_vma=False,
    )
```

```python
import numpy as np

import jax
import jax.numpy as jnp
from jax import lax
from jax.experimental import pallas as pl
from jax.experimental.pallas import tpu as pltpu
from jax.sharding import PartitionSpec as P

ORDER = 8


epsilon = 1e-06


def tables(points, sources, depth):
    block = 32
    index = jnp.arange(points, dtype=jnp.int32)
    step = jnp.arange(block, dtype=jnp.int32)
    factor = jnp.float32(points ** (-0.5))
    scale = jnp.float32(2.0 * np.pi / points)
    high = ((block * step)[:, None] * index[None, :]) % points
    low = (step[:, None] * index[None, :]) % points
    high_c = jnp.cos(scale * high.astype(jnp.float32))
    high_s = jnp.sin(scale * high.astype(jnp.float32))
    low_c = jnp.cos(scale * low.astype(jnp.float32))
    low_s = jnp.sin(scale * low.astype(jnp.float32))
    cos = high_c[:, None, :] * low_c[None, :, :] - high_s[:, None, :] * low_s[None, :, :]
    sin = high_s[:, None, :] * low_c[None, :, :] + high_c[:, None, :] * low_s[None, :, :]
    cos = (cos * factor).astype(jnp.bfloat16).reshape(points, points)
    sin = (sin * factor).astype(jnp.bfloat16).reshape(points, points)

    def spread(x):
        x = x.reshape(block, sources, 1, depth)
        return jnp.concatenate([x, x], axis=2).reshape(block, sources * 2 * depth)

    part = (jnp.arange(sources * 2 * depth, dtype=jnp.int32) // depth) % 2 == 0
    hc, hs, lc, ls = spread(high_c), spread(high_s), spread(low_c), spread(low_s)
    first = jnp.where(part[None, :], hc, -hs)
    second = jnp.where(part[None, :], -hs, -hc)
    table = first[:, None, :] * lc[None, :, :] + second[:, None, :] * ls[None, :, :]
    table = (table * factor).astype(jnp.bfloat16).reshape(points, sources * 2 * depth)
    return lax.optimization_barrier((cos, sin)) + (lax.optimization_barrier(table),)


def distances(row_pos, col_pos, points):
    half = jnp.float32(points / 2.0)
    row_term = (row_pos - half) * (row_pos - half)
    col_term = (col_pos - half) * (col_pos - half)
    return (row_term[:, None] + col_term[None, :]) / (half * half)


def basis_rows(channels, degree):
    abscissa = (2.0 * np.arange(channels, dtype=np.float64) - (channels - 1)) / (channels - 1)
    legendre = [np.ones((channels,), np.float64), abscissa]
    for order_idx in range(1, degree):
        legendre.append(
            (
                (2 * order_idx + 1) * abscissa * legendre[order_idx]
                - order_idx * legendre[order_idx - 1]
            )
            / (order_idx + 1)
        )
    legendre = legendre[: degree + 1]
    rows = []
    for vector in legendre:
        for sweep in range(2):
            for earlier in rows:
                vector = vector - np.sum(vector * earlier) * earlier
        vector = vector / np.sqrt(np.sum(vector * vector))
        rows.append(vector)
    return np.stack(rows).astype(np.float32)


def filters(templates, channels, degree):
    basis = jnp.asarray(basis_rows(channels, degree))
    coeffs = jnp.dot(templates, basis.T, precision=lax.Precision.HIGHEST)
    matched = templates - jnp.dot(coeffs, basis, precision=lax.Precision.HIGHEST)
    return jnp.concatenate([matched, basis], axis=0).astype(jnp.bfloat16)


def send_kernel(cos_ref, sin_ref, out_ref):
    channels = cos_ref.shape[0]
    points = cos_ref.shape[3]
    lanes = 128
    width = out_ref.shape[3] // channels
    per_vreg = lanes // width
    real = cos_ref[:, 0] - sin_ref[:, 1]
    imag = sin_ref[:, 0] + cos_ref[:, 1]
    lane_group = lax.broadcasted_iota(jnp.int32, (real.shape[1], lanes), 1) // width
    for t in range(points // lanes):
        for p, part in enumerate((real, imag)):
            block = part[:, :, t * lanes:(t + 1) * lanes]
            for q in range(per_vreg):
                for h in range(channels // per_vreg):
                    acc = jnp.zeros(block.shape[1:], jnp.float32)
                    for j in range(per_vreg):
                        shift = (width * (j - q)) % lanes
                        piece = block[h * per_vreg + j]
                        if shift:
                            piece = pltpu.roll(piece, shift, 1)
                        acc = jnp.where(lane_group == j, piece, acc)
                    out_ref[t * per_vreg + q, p, :, h * lanes:(h + 1) * lanes] = acc.astype(
                        out_ref.dtype
                    )


def make_send(with_cos, with_sin, sky_count, columns):
    channels, _, row_count, points = with_cos.shape
    rows = 8
    spec_in = pl.BlockSpec((channels, 2, rows, points), lambda r: (0, 0, r, 0))
    return pl.pallas_call(
        send_kernel,
        grid=(row_count // rows,),
        in_specs=[spec_in, spec_in],
        out_specs=pl.BlockSpec(
            (sky_count, 2, rows, channels * columns), lambda r: (0, 0, r, 0)
        ),
        out_shape=jax.ShapeDtypeStruct(
            (sky_count, 2, row_count, channels * columns), jnp.bfloat16
        ),
        cost_estimate=pl.CostEstimate(
            flops=2 * with_cos.size, transcendentals=0, bytes_accessed=5 * with_cos.size
        ),
    )(with_cos, with_sin)


def image_kernel(table_ref, turned_ref, rate_ref, across_ref, out_ref, power_ref):
    step = pl.program_id(0)
    tile = table_ref.shape[0]
    lines = out_ref.shape[1] - 1
    per_tile = tile // lines
    points = tile * pl.num_programs(0)
    half = jnp.float32(points / 2.0)
    picture = jnp.dot(table_ref[...], turned_ref[...], preferred_element_type=jnp.float32)
    row = (lax.broadcasted_iota(jnp.int32, picture.shape, 0) + step * tile).astype(jnp.float32)
    row_term = (row - half) * (row - half)
    dist = (row_term + across_ref[...]) / (half * half)
    image = (jnp.exp(rate_ref[...] * dist) * picture).astype(out_ref.dtype)
    for k in range(per_tile):
        out_ref[pl.ds(step * per_tile + k, 1), pl.ds(0, lines), :] = image[
            k * lines:(k + 1) * lines
        ][None]
    widened = image.astype(jnp.float32)
    partial = jnp.sum(widened * widened, axis=0, keepdims=True)

    @pl.when(step == 0)
    def _():
        power_ref[...] = jnp.zeros_like(power_ref)

    power_ref[...] += partial

    @pl.when(step == pl.num_programs(0) - 1)
    def _():
        total = jnp.sum(power_ref[...], axis=1, keepdims=True)
        high = total.astype(out_ref.dtype)
        rest = total - high.astype(jnp.float32)
        middle = rest.astype(out_ref.dtype)
        low = (rest - middle.astype(jnp.float32)).astype(out_ref.dtype)
        lane = lax.broadcasted_iota(jnp.int32, power_ref.shape, 1)
        zero = jnp.zeros(power_ref.shape, out_ref.dtype)
        pieces = jnp.where(
            lane == 0, high, jnp.where(lane == 1, middle, jnp.where(lane == 2, low, zero))
        )
        for f in range(out_ref.shape[0]):
            out_ref[pl.ds(f, 1), pl.ds(lines, 1), :] = pieces[None]


def make_images(table, turned, rate, across, freq_count):
    points, depth = table.shape
    width = turned.shape[1]
    lines = points // freq_count
    tile = 256
    return pl.pallas_call(
        image_kernel,
        grid=(points // tile,),
        in_specs=[
            pl.BlockSpec((tile, depth), lambda i: (i, 0)),
            pl.BlockSpec((depth, width), lambda i: (0, 0)),
            pl.BlockSpec((1, width), lambda i: (0, 0)),
            pl.BlockSpec((1, width), lambda i: (0, 0)),
        ],
        out_specs=pl.BlockSpec((freq_count, lines + 1, width), lambda i: (0, 0, 0)),
        out_shape=jax.ShapeDtypeStruct((freq_count, lines + 1, width), jnp.bfloat16),
        scratch_shapes=[pltpu.VMEM((1, width), jnp.float32)],
        cost_estimate=pl.CostEstimate(
            flops=2 * points * depth * width,
            transcendentals=points * width,
            bytes_accessed=2 * (points * depth + depth * width + points * width),
        ),
    )(table, turned, rate, across)


def body(visibilities, templates):
    channels = visibilities.shape[0]
    row_count = visibilities.shape[2]
    points = visibilities.shape[3]
    num_templates = templates.shape[0]
    freq_count = lax.axis_size("freq")
    sky_count = lax.axis_size("sky")
    all_channels = channels * freq_count
    columns = points // sky_count
    lines = points // freq_count
    cosine, sine, table = tables(points, sky_count, row_count)

    rows = visibilities.reshape(channels * 2 * row_count, points)
    with_cos = jnp.dot(rows, cosine, preferred_element_type=jnp.float32).reshape(
        channels, 2, row_count, points
    )
    with_sin = jnp.dot(rows, sine, preferred_element_type=jnp.float32).reshape(
        channels, 2, row_count, points
    )
    send = make_send(with_cos, with_sin, sky_count, columns)
    turned = lax.all_to_all(send, "sky", 0, 0, tiled=True)
    turned = turned.reshape(sky_count * 2 * row_count, channels * columns)

    col_pos = (lax.axis_index("sky") * columns + jnp.arange(columns, dtype=jnp.int32)).astype(
        jnp.float32
    )
    chan_pos = (lax.axis_index("freq") * channels + jnp.arange(channels, dtype=jnp.int32)).astype(
        jnp.float32
    )
    stretch = 1.0 + 0.5 * chan_pos / jnp.float32(all_channels - 1)
    coef = -0.7 * stretch * stretch
    half = jnp.float32(points / 2.0)
    rate = jnp.broadcast_to(coef[:, None], (channels, columns)).reshape(1, channels * columns)
    across = jnp.broadcast_to(
        ((col_pos - half) * (col_pos - half))[None, :], (channels, columns)
    ).reshape(1, channels * columns)
    outgoing = make_images(table, turned, rate, across, freq_count)
    gathered = lax.all_to_all(outgoing, "freq", 0, 0, tiled=True)
    power_freq = jnp.sum(gathered[:, lines, :3].astype(jnp.float32))
    column_power = lax.all_to_all(
        jnp.broadcast_to(power_freq, (sky_count, 128)), "sky", 0, 0, tiled=True
    )
    power_sum = jnp.sum(column_power[:, 0])
    images = gathered[:, :lines].reshape(freq_count, lines, channels, columns)
    weights = filters(templates, all_channels, ORDER).reshape(-1, freq_count, channels)
    result = jnp.einsum(
        "kfc,flcm->klm", weights, images, preferred_element_type=jnp.float32
    )
    spread = jnp.sqrt(power_sum / (all_channels * points * points) + epsilon)
    return (result[:num_templates] / spread, result[num_templates:])


def solution(mesh):
    return jax.shard_map(
        body,
        mesh=mesh,
        in_specs=(P("freq", None, "sky", None), P()),
        out_specs=(P(None, "freq", "sky"), P(None, "freq", "sky")),
        check_vma=False,
    )
```

```python
import numpy as np

import jax
import jax.numpy as jnp
from jax import lax
from jax.experimental import pallas as pl
from jax.experimental.pallas import tpu as pltpu
from jax.sharding import PartitionSpec as P

ORDER = 8


epsilon = 1e-06


def tables(points, sources, depth):
    block = 32
    index = jnp.arange(points, dtype=jnp.int32)
    step = jnp.arange(block, dtype=jnp.int32)
    factor = jnp.float32(points ** (-0.5))
    scale = jnp.float32(2.0 * np.pi / points)
    high = ((block * step)[:, None] * index[None, :]) % points
    low = (step[:, None] * index[None, :]) % points
    high_c = jnp.cos(scale * high.astype(jnp.float32))
    high_s = jnp.sin(scale * high.astype(jnp.float32))
    low_c = jnp.cos(scale * low.astype(jnp.float32))
    low_s = jnp.sin(scale * low.astype(jnp.float32))
    cos = high_c[:, None, :] * low_c[None, :, :] - high_s[:, None, :] * low_s[None, :, :]
    sin = high_s[:, None, :] * low_c[None, :, :] + high_c[:, None, :] * low_s[None, :, :]
    cos = (cos * factor).astype(jnp.bfloat16).reshape(points, points)
    sin = (sin * factor).astype(jnp.bfloat16).reshape(points, points)

    def spread(x):
        x = x.reshape(block, sources, 1, depth)
        return jnp.concatenate([x, x], axis=2).reshape(block, sources * 2 * depth)

    part = (jnp.arange(sources * 2 * depth, dtype=jnp.int32) // depth) % 2 == 0
    hc, hs, lc, ls = spread(high_c), spread(high_s), spread(low_c), spread(low_s)
    first = jnp.where(part[None, :], hc, -hs)
    second = jnp.where(part[None, :], -hs, -hc)
    table = first[:, None, :] * lc[None, :, :] + second[:, None, :] * ls[None, :, :]
    table = (table * factor).astype(jnp.bfloat16).reshape(points, sources * 2 * depth)
    return lax.optimization_barrier((cos, sin)) + (lax.optimization_barrier(table),)


def distances(row_pos, col_pos, points):
    half = jnp.float32(points / 2.0)
    row_term = (row_pos - half) * (row_pos - half)
    col_term = (col_pos - half) * (col_pos - half)
    return (row_term[:, None] + col_term[None, :]) / (half * half)


def basis_rows(channels, degree):
    abscissa = (2.0 * np.arange(channels, dtype=np.float64) - (channels - 1)) / (channels - 1)
    legendre = [np.ones((channels,), np.float64), abscissa]
    for order_idx in range(1, degree):
        legendre.append(
            (
                (2 * order_idx + 1) * abscissa * legendre[order_idx]
                - order_idx * legendre[order_idx - 1]
            )
            / (order_idx + 1)
        )
    legendre = legendre[: degree + 1]
    rows = []
    for vector in legendre:
        for sweep in range(2):
            for earlier in rows:
                vector = vector - np.sum(vector * earlier) * earlier
        vector = vector / np.sqrt(np.sum(vector * vector))
        rows.append(vector)
    return np.stack(rows).astype(np.float32)


def filters(templates, channels, degree):
    basis = jnp.asarray(basis_rows(channels, degree))
    coeffs = jnp.dot(templates, basis.T, precision=lax.Precision.HIGHEST)
    matched = templates - jnp.dot(coeffs, basis, precision=lax.Precision.HIGHEST)
    return jnp.concatenate([matched, basis], axis=0).astype(jnp.bfloat16)


def send_kernel(cos_ref, sin_ref, out_ref):
    channels = cos_ref.shape[0]
    points = cos_ref.shape[3]
    lanes = 128
    width = out_ref.shape[3] // channels
    per_vreg = lanes // width
    real = cos_ref[:, 0] - sin_ref[:, 1]
    imag = sin_ref[:, 0] + cos_ref[:, 1]
    lane_group = lax.broadcasted_iota(jnp.int32, (real.shape[1], lanes), 1) // width
    for t in range(points // lanes):
        for p, part in enumerate((real, imag)):
            block = part[:, :, t * lanes:(t + 1) * lanes]
            for q in range(per_vreg):
                for h in range(channels // per_vreg):
                    acc = jnp.zeros(block.shape[1:], jnp.float32)
                    for j in range(per_vreg):
                        shift = (width * (j - q)) % lanes
                        piece = block[h * per_vreg + j]
                        if shift:
                            piece = pltpu.roll(piece, shift, 1)
                        acc = jnp.where(lane_group == j, piece, acc)
                    out_ref[t * per_vreg + q, p, :, h * lanes:(h + 1) * lanes] = acc.astype(
                        out_ref.dtype
                    )


def make_send(with_cos, with_sin, sky_count, columns):
    channels, _, row_count, points = with_cos.shape
    rows = 8
    spec_in = pl.BlockSpec((channels, 2, rows, points), lambda r: (0, 0, r, 0))
    return pl.pallas_call(
        send_kernel,
        grid=(row_count // rows,),
        in_specs=[spec_in, spec_in],
        out_specs=pl.BlockSpec(
            (sky_count, 2, rows, channels * columns), lambda r: (0, 0, r, 0)
        ),
        out_shape=jax.ShapeDtypeStruct(
            (sky_count, 2, row_count, channels * columns), jnp.bfloat16
        ),
        cost_estimate=pl.CostEstimate(
            flops=2 * with_cos.size, transcendentals=0, bytes_accessed=5 * with_cos.size
        ),
    )(with_cos, with_sin)


def image_kernel(table_ref, turned_ref, rate_ref, across_ref, out_ref, power_ref):
    step = pl.program_id(0)
    tile = table_ref.shape[0]
    lines = out_ref.shape[1] - 1
    per_tile = tile // lines
    points = tile * pl.num_programs(0)
    half = jnp.float32(points / 2.0)
    picture = jnp.dot(table_ref[...], turned_ref[...], preferred_element_type=jnp.float32)
    row = (lax.broadcasted_iota(jnp.int32, picture.shape, 0) + step * tile).astype(jnp.float32)
    row_term = (row - half) * (row - half)
    dist = (row_term + across_ref[...]) / (half * half)
    image = (jnp.exp(rate_ref[...] * dist) * picture).astype(out_ref.dtype)
    for k in range(per_tile):
        out_ref[pl.ds(step * per_tile + k, 1), pl.ds(0, lines), :] = image[
            k * lines:(k + 1) * lines
        ][None]
    widened = image.astype(jnp.float32)
    partial = jnp.sum(widened * widened, axis=0, keepdims=True)

    @pl.when(step == 0)
    def _():
        power_ref[...] = jnp.zeros_like(power_ref)

    power_ref[...] += partial

    @pl.when(step == pl.num_programs(0) - 1)
    def _():
        total = jnp.sum(power_ref[...], axis=1, keepdims=True)
        high = total.astype(out_ref.dtype)
        rest = total - high.astype(jnp.float32)
        middle = rest.astype(out_ref.dtype)
        low = (rest - middle.astype(jnp.float32)).astype(out_ref.dtype)
        lane = lax.broadcasted_iota(jnp.int32, power_ref.shape, 1)
        zero = jnp.zeros(power_ref.shape, out_ref.dtype)
        pieces = jnp.where(
            lane == 0, high, jnp.where(lane == 1, middle, jnp.where(lane == 2, low, zero))
        )
        for f in range(out_ref.shape[0]):
            out_ref[pl.ds(f, 1), pl.ds(lines, 1), :] = pieces[None]


def make_images(table, turned, rate, across, freq_count):
    points, depth = table.shape
    width = turned.shape[1]
    lines = points // freq_count
    tile = 256
    return pl.pallas_call(
        image_kernel,
        grid=(points // tile,),
        in_specs=[
            pl.BlockSpec((tile, depth), lambda i: (i, 0)),
            pl.BlockSpec((depth, width), lambda i: (0, 0)),
            pl.BlockSpec((1, width), lambda i: (0, 0)),
            pl.BlockSpec((1, width), lambda i: (0, 0)),
        ],
        out_specs=pl.BlockSpec((freq_count, lines + 1, width), lambda i: (0, 0, 0)),
        out_shape=jax.ShapeDtypeStruct((freq_count, lines + 1, width), jnp.bfloat16),
        scratch_shapes=[pltpu.VMEM((1, width), jnp.float32)],
        cost_estimate=pl.CostEstimate(
            flops=2 * points * depth * width,
            transcendentals=points * width,
            bytes_accessed=2 * (points * depth + depth * width + points * width),
        ),
    )(table, turned, rate, across)


def body(visibilities, templates):
    channels = visibilities.shape[0]
    row_count = visibilities.shape[2]
    points = visibilities.shape[3]
    num_templates = templates.shape[0]
    freq_count = lax.axis_size("freq")
    sky_count = lax.axis_size("sky")
    all_channels = channels * freq_count
    columns = points // sky_count
    lines = points // freq_count
    cosine, sine, table = tables(points, sky_count, row_count)

    rows = visibilities.reshape(channels * 2 * row_count, points)
    with_cos = jnp.dot(rows, cosine, preferred_element_type=jnp.float32).reshape(
        channels, 2, row_count, points
    )
    with_sin = jnp.dot(rows, sine, preferred_element_type=jnp.float32).reshape(
        channels, 2, row_count, points
    )
    send = make_send(with_cos, with_sin, sky_count, columns)
    turned = lax.all_to_all(send, "sky", 0, 0, tiled=True)
    turned = turned.reshape(sky_count * 2 * row_count, channels * columns)

    col_pos = (lax.axis_index("sky") * columns + jnp.arange(columns, dtype=jnp.int32)).astype(
        jnp.float32
    )
    chan_pos = (lax.axis_index("freq") * channels + jnp.arange(channels, dtype=jnp.int32)).astype(
        jnp.float32
    )
    stretch = 1.0 + 0.5 * chan_pos / jnp.float32(all_channels - 1)
    coef = -0.7 * stretch * stretch
    half = jnp.float32(points / 2.0)
    rate = jnp.broadcast_to(coef[:, None], (channels, columns)).reshape(1, channels * columns)
    across = jnp.broadcast_to(
        ((col_pos - half) * (col_pos - half))[None, :], (channels, columns)
    ).reshape(1, channels * columns)
    outgoing = make_images(table, turned, rate, across, freq_count)
    gathered = lax.all_to_all(outgoing, "freq", 0, 0, tiled=True)
    power_freq = jnp.sum(gathered[:, lines, :3].astype(jnp.float32))
    column_power = lax.all_to_all(
        jnp.broadcast_to(power_freq, (sky_count, 8, 128)), "sky", 0, 0, tiled=True
    )
    power_sum = jnp.sum(column_power[:, 0, 0])
    images = gathered[:, :lines].reshape(freq_count, lines, channels, columns)
    weights = filters(templates, all_channels, ORDER).reshape(-1, freq_count, channels)
    result = jnp.einsum(
        "kfc,flcm->klm", weights, images, preferred_element_type=jnp.float32
    )
    spread = jnp.sqrt(power_sum / (all_channels * points * points) + epsilon)
    return (result[:num_templates] / spread, result[num_templates:])


def solution(mesh):
    return jax.shard_map(
        body,
        mesh=mesh,
        in_specs=(P("freq", None, "sky", None), P()),
        out_specs=(P(None, "freq", "sky"), P(None, "freq", "sky")),
        check_vma=False,
    )
```

```python
import numpy as np

import jax
import jax.numpy as jnp
from jax import lax
from jax.experimental import pallas as pl
from jax.experimental.pallas import tpu as pltpu
from jax.sharding import PartitionSpec as P

ORDER = 8


epsilon = 1e-06


def tables(points, sources, depth):
    block = 32
    index = jnp.arange(points, dtype=jnp.int32)
    step = jnp.arange(block, dtype=jnp.int32)
    factor = jnp.float32(points ** (-0.5))
    scale = jnp.float32(2.0 * np.pi / points)
    high = ((block * step)[:, None] * index[None, :]) % points
    low = (step[:, None] * index[None, :]) % points
    high_c = jnp.cos(scale * high.astype(jnp.float32))
    high_s = jnp.sin(scale * high.astype(jnp.float32))
    low_c = jnp.cos(scale * low.astype(jnp.float32))
    low_s = jnp.sin(scale * low.astype(jnp.float32))
    cos = high_c[:, None, :] * low_c[None, :, :] - high_s[:, None, :] * low_s[None, :, :]
    sin = high_s[:, None, :] * low_c[None, :, :] + high_c[:, None, :] * low_s[None, :, :]
    cos = (cos * factor).astype(jnp.bfloat16).reshape(points, points)
    sin = (sin * factor).astype(jnp.bfloat16).reshape(points, points)

    def spread(x):
        x = x.reshape(block, sources, 1, depth)
        return jnp.concatenate([x, x], axis=2).reshape(block, sources * 2 * depth)

    part = (jnp.arange(sources * 2 * depth, dtype=jnp.int32) // depth) % 2 == 0
    hc, hs, lc, ls = spread(high_c), spread(high_s), spread(low_c), spread(low_s)
    first = jnp.where(part[None, :], hc, -hs)
    second = jnp.where(part[None, :], -hs, -hc)
    table = first[:, None, :] * lc[None, :, :] + second[:, None, :] * ls[None, :, :]
    table = (table * factor).astype(jnp.bfloat16).reshape(points, sources * 2 * depth)
    return lax.optimization_barrier((cos, sin)) + (lax.optimization_barrier(table),)


def distances(row_pos, col_pos, points):
    half = jnp.float32(points / 2.0)
    row_term = (row_pos - half) * (row_pos - half)
    col_term = (col_pos - half) * (col_pos - half)
    return (row_term[:, None] + col_term[None, :]) / (half * half)


def basis_rows(channels, degree):
    abscissa = (2.0 * np.arange(channels, dtype=np.float64) - (channels - 1)) / (channels - 1)
    legendre = [np.ones((channels,), np.float64), abscissa]
    for order_idx in range(1, degree):
        legendre.append(
            (
                (2 * order_idx + 1) * abscissa * legendre[order_idx]
                - order_idx * legendre[order_idx - 1]
            )
            / (order_idx + 1)
        )
    legendre = legendre[: degree + 1]
    rows = []
    for vector in legendre:
        for sweep in range(2):
            for earlier in rows:
                vector = vector - np.sum(vector * earlier) * earlier
        vector = vector / np.sqrt(np.sum(vector * vector))
        rows.append(vector)
    return np.stack(rows).astype(np.float32)


def filters(templates, channels, degree):
    basis = jnp.asarray(basis_rows(channels, degree))
    coeffs = jnp.dot(templates, basis.T, precision=lax.Precision.HIGHEST)
    matched = templates - jnp.dot(coeffs, basis, precision=lax.Precision.HIGHEST)
    return jnp.concatenate([matched, basis], axis=0).astype(jnp.bfloat16)


def send_kernel(cos_ref, sin_ref, out_ref):
    channels = cos_ref.shape[0]
    points = cos_ref.shape[3]
    lanes = 128
    width = out_ref.shape[3] // channels
    per_vreg = lanes // width
    real = cos_ref[:, 0] - sin_ref[:, 1]
    imag = sin_ref[:, 0] + cos_ref[:, 1]
    lane_group = lax.broadcasted_iota(jnp.int32, (real.shape[1], lanes), 1) // width
    for t in range(points // lanes):
        for p, part in enumerate((real, imag)):
            block = part[:, :, t * lanes:(t + 1) * lanes]
            for q in range(per_vreg):
                for h in range(channels // per_vreg):
                    acc = jnp.zeros(block.shape[1:], jnp.float32)
                    for j in range(per_vreg):
                        shift = (width * (j - q)) % lanes
                        piece = block[h * per_vreg + j]
                        if shift:
                            piece = pltpu.roll(piece, shift, 1)
                        acc = jnp.where(lane_group == j, piece, acc)
                    out_ref[t * per_vreg + q, p, :, h * lanes:(h + 1) * lanes] = acc.astype(
                        out_ref.dtype
                    )


def make_send(with_cos, with_sin, sky_count, columns):
    channels, _, row_count, points = with_cos.shape
    rows = 8
    spec_in = pl.BlockSpec((channels, 2, rows, points), lambda r: (0, 0, r, 0))
    return pl.pallas_call(
        send_kernel,
        grid=(row_count // rows,),
        in_specs=[spec_in, spec_in],
        out_specs=pl.BlockSpec(
            (sky_count, 2, rows, channels * columns), lambda r: (0, 0, r, 0)
        ),
        out_shape=jax.ShapeDtypeStruct(
            (sky_count, 2, row_count, channels * columns), jnp.bfloat16
        ),
        cost_estimate=pl.CostEstimate(
            flops=2 * with_cos.size, transcendentals=0, bytes_accessed=5 * with_cos.size
        ),
    )(with_cos, with_sin)


def image_kernel(table_ref, turned_ref, rate_ref, across_ref, out_ref, power_ref):
    step = pl.program_id(0)
    tile = table_ref.shape[0]
    lines = out_ref.shape[1] - 1
    per_tile = tile // lines
    points = tile * pl.num_programs(0)
    half = jnp.float32(points / 2.0)
    picture = jnp.dot(table_ref[...], turned_ref[...], preferred_element_type=jnp.float32)
    row = (lax.broadcasted_iota(jnp.int32, picture.shape, 0) + step * tile).astype(jnp.float32)
    row_term = (row - half) * (row - half)
    dist = (row_term + across_ref[...]) / (half * half)
    image = (jnp.exp(rate_ref[...] * dist) * picture).astype(out_ref.dtype)
    for k in range(per_tile):
        out_ref[pl.ds(step * per_tile + k, 1), pl.ds(0, lines), :] = image[
            k * lines:(k + 1) * lines
        ][None]
    widened = image.astype(jnp.float32)
    partial = jnp.sum(widened * widened, axis=0, keepdims=True)

    @pl.when(step == 0)
    def _():
        power_ref[...] = jnp.zeros_like(power_ref)

    power_ref[...] += partial

    @pl.when(step == pl.num_programs(0) - 1)
    def _():
        total = jnp.sum(power_ref[...], axis=1, keepdims=True)
        high = total.astype(out_ref.dtype)
        rest = total - high.astype(jnp.float32)
        middle = rest.astype(out_ref.dtype)
        low = (rest - middle.astype(jnp.float32)).astype(out_ref.dtype)
        lane = lax.broadcasted_iota(jnp.int32, power_ref.shape, 1)
        zero = jnp.zeros(power_ref.shape, out_ref.dtype)
        pieces = jnp.where(
            lane == 0, high, jnp.where(lane == 1, middle, jnp.where(lane == 2, low, zero))
        )
        for f in range(out_ref.shape[0]):
            out_ref[pl.ds(f, 1), pl.ds(lines, 1), :] = pieces[None]


def make_images(table, turned, rate, across, freq_count):
    points, depth = table.shape
    width = turned.shape[1]
    lines = points // freq_count
    tile = 512
    return pl.pallas_call(
        image_kernel,
        grid=(points // tile,),
        in_specs=[
            pl.BlockSpec((tile, depth), lambda i: (i, 0)),
            pl.BlockSpec((depth, width), lambda i: (0, 0)),
            pl.BlockSpec((1, width), lambda i: (0, 0)),
            pl.BlockSpec((1, width), lambda i: (0, 0)),
        ],
        out_specs=pl.BlockSpec((freq_count, lines + 1, width), lambda i: (0, 0, 0)),
        out_shape=jax.ShapeDtypeStruct((freq_count, lines + 1, width), jnp.bfloat16),
        scratch_shapes=[pltpu.VMEM((1, width), jnp.float32)],
        cost_estimate=pl.CostEstimate(
            flops=2 * points * depth * width,
            transcendentals=points * width,
            bytes_accessed=2 * (points * depth + depth * width + points * width),
        ),
    )(table, turned, rate, across)


def body(visibilities, templates):
    channels = visibilities.shape[0]
    row_count = visibilities.shape[2]
    points = visibilities.shape[3]
    num_templates = templates.shape[0]
    freq_count = lax.axis_size("freq")
    sky_count = lax.axis_size("sky")
    all_channels = channels * freq_count
    columns = points // sky_count
    lines = points // freq_count
    cosine, sine, table = tables(points, sky_count, row_count)

    rows = visibilities.reshape(channels * 2 * row_count, points)
    with_cos = jnp.dot(rows, cosine, preferred_element_type=jnp.float32).reshape(
        channels, 2, row_count, points
    )
    with_sin = jnp.dot(rows, sine, preferred_element_type=jnp.float32).reshape(
        channels, 2, row_count, points
    )
    send = make_send(with_cos, with_sin, sky_count, columns)
    turned = lax.all_to_all(send, "sky", 0, 0, tiled=True)
    turned = turned.reshape(sky_count * 2 * row_count, channels * columns)

    col_pos = (lax.axis_index("sky") * columns + jnp.arange(columns, dtype=jnp.int32)).astype(
        jnp.float32
    )
    chan_pos = (lax.axis_index("freq") * channels + jnp.arange(channels, dtype=jnp.int32)).astype(
        jnp.float32
    )
    stretch = 1.0 + 0.5 * chan_pos / jnp.float32(all_channels - 1)
    coef = -0.7 * stretch * stretch
    half = jnp.float32(points / 2.0)
    rate = jnp.broadcast_to(coef[:, None], (channels, columns)).reshape(1, channels * columns)
    across = jnp.broadcast_to(
        ((col_pos - half) * (col_pos - half))[None, :], (channels, columns)
    ).reshape(1, channels * columns)
    outgoing = make_images(table, turned, rate, across, freq_count)
    gathered = lax.all_to_all(outgoing, "freq", 0, 0, tiled=True)
    power_freq = jnp.sum(gathered[:, lines, :3].astype(jnp.float32))
    column_power = lax.all_to_all(
        jnp.broadcast_to(power_freq, (sky_count, 128)), "sky", 0, 0, tiled=True
    )
    power_sum = jnp.sum(column_power[:, 0])
    images = gathered[:, :lines].reshape(freq_count, lines, channels, columns)
    weights = filters(templates, all_channels, ORDER).reshape(-1, freq_count, channels)
    result = jnp.einsum(
        "kfc,flcm->klm", weights, images, preferred_element_type=jnp.float32
    )
    spread = jnp.sqrt(power_sum / (all_channels * points * points) + epsilon)
    return (result[:num_templates] / spread, result[num_templates:])


def solution(mesh):
    return jax.shard_map(
        body,
        mesh=mesh,
        in_specs=(P("freq", None, "sky", None), P()),
        out_specs=(P(None, "freq", "sky"), P(None, "freq", "sky")),
        check_vma=False,
    )
```

```python
import numpy as np

import jax
import jax.numpy as jnp
from jax import lax
from jax.experimental import pallas as pl
from jax.experimental.pallas import tpu as pltpu
from jax.sharding import PartitionSpec as P

ORDER = 8


epsilon = 1e-06


def tables(points, sources, depth):
    block = 32
    index = jnp.arange(points, dtype=jnp.int32)
    step = jnp.arange(block, dtype=jnp.int32)
    factor = jnp.float32(points ** (-0.5))
    scale = jnp.float32(2.0 * np.pi / points)
    high = ((block * step)[:, None] * index[None, :]) % points
    low = (step[:, None] * index[None, :]) % points
    high_c = jnp.cos(scale * high.astype(jnp.float32))
    high_s = jnp.sin(scale * high.astype(jnp.float32))
    low_c = jnp.cos(scale * low.astype(jnp.float32))
    low_s = jnp.sin(scale * low.astype(jnp.float32))
    cos = high_c[:, None, :] * low_c[None, :, :] - high_s[:, None, :] * low_s[None, :, :]
    sin = high_s[:, None, :] * low_c[None, :, :] + high_c[:, None, :] * low_s[None, :, :]
    cos = (cos * factor).astype(jnp.bfloat16).reshape(points, points)
    sin = (sin * factor).astype(jnp.bfloat16).reshape(points, points)

    def spread(x):
        x = x.reshape(block, sources, 1, depth)
        return jnp.concatenate([x, x], axis=2).reshape(block, sources * 2 * depth)

    part = (jnp.arange(sources * 2 * depth, dtype=jnp.int32) // depth) % 2 == 0
    hc, hs, lc, ls = spread(high_c), spread(high_s), spread(low_c), spread(low_s)
    first = jnp.where(part[None, :], hc, -hs)
    second = jnp.where(part[None, :], -hs, -hc)
    table = first[:, None, :] * lc[None, :, :] + second[:, None, :] * ls[None, :, :]
    table = (table * factor).astype(jnp.bfloat16).reshape(points, sources * 2 * depth)
    return lax.optimization_barrier((cos, sin)) + (lax.optimization_barrier(table),)


def distances(row_pos, col_pos, points):
    half = jnp.float32(points / 2.0)
    row_term = (row_pos - half) * (row_pos - half)
    col_term = (col_pos - half) * (col_pos - half)
    return (row_term[:, None] + col_term[None, :]) / (half * half)


def basis_rows(channels, degree):
    abscissa = (2.0 * np.arange(channels, dtype=np.float64) - (channels - 1)) / (channels - 1)
    legendre = [np.ones((channels,), np.float64), abscissa]
    for order_idx in range(1, degree):
        legendre.append(
            (
                (2 * order_idx + 1) * abscissa * legendre[order_idx]
                - order_idx * legendre[order_idx - 1]
            )
            / (order_idx + 1)
        )
    legendre = legendre[: degree + 1]
    rows = []
    for vector in legendre:
        for sweep in range(2):
            for earlier in rows:
                vector = vector - np.sum(vector * earlier) * earlier
        vector = vector / np.sqrt(np.sum(vector * vector))
        rows.append(vector)
    return np.stack(rows).astype(np.float32)


def filters(templates, channels, degree):
    basis = jnp.asarray(basis_rows(channels, degree))
    coeffs = jnp.dot(templates, basis.T, precision=lax.Precision.HIGHEST)
    matched = templates - jnp.dot(coeffs, basis, precision=lax.Precision.HIGHEST)
    return jnp.concatenate([matched, basis], axis=0).astype(jnp.bfloat16)


def send_kernel(cos_ref, sin_ref, out_ref):
    channels = cos_ref.shape[0]
    points = cos_ref.shape[3]
    lanes = 128
    width = out_ref.shape[3] // channels
    per_vreg = lanes // width
    real = cos_ref[:, 0] - sin_ref[:, 1]
    imag = sin_ref[:, 0] + cos_ref[:, 1]
    lane_group = lax.broadcasted_iota(jnp.int32, (real.shape[1], lanes), 1) // width
    for t in range(points // lanes):
        for p, part in enumerate((real, imag)):
            block = part[:, :, t * lanes:(t + 1) * lanes]
            for q in range(per_vreg):
                for h in range(channels // per_vreg):
                    acc = jnp.zeros(block.shape[1:], jnp.float32)
                    for j in range(per_vreg):
                        shift = (width * (j - q)) % lanes
                        piece = block[h * per_vreg + j]
                        if shift:
                            piece = pltpu.roll(piece, shift, 1)
                        acc = jnp.where(lane_group == j, piece, acc)
                    out_ref[t * per_vreg + q, p, :, h * lanes:(h + 1) * lanes] = acc.astype(
                        out_ref.dtype
                    )


def make_send(with_cos, with_sin, sky_count, columns):
    channels, _, row_count, points = with_cos.shape
    rows = 16
    spec_in = pl.BlockSpec((channels, 2, rows, points), lambda r: (0, 0, r, 0))
    return pl.pallas_call(
        send_kernel,
        grid=(row_count // rows,),
        in_specs=[spec_in, spec_in],
        out_specs=pl.BlockSpec(
            (sky_count, 2, rows, channels * columns), lambda r: (0, 0, r, 0)
        ),
        out_shape=jax.ShapeDtypeStruct(
            (sky_count, 2, row_count, channels * columns), jnp.bfloat16
        ),
        cost_estimate=pl.CostEstimate(
            flops=2 * with_cos.size, transcendentals=0, bytes_accessed=5 * with_cos.size
        ),
    )(with_cos, with_sin)


def image_kernel(table_ref, turned_ref, rate_ref, across_ref, out_ref, power_ref):
    step = pl.program_id(0)
    tile = table_ref.shape[0]
    lines = out_ref.shape[1] - 1
    per_tile = tile // lines
    points = tile * pl.num_programs(0)
    half = jnp.float32(points / 2.0)
    picture = jnp.dot(table_ref[...], turned_ref[...], preferred_element_type=jnp.float32)
    row = (lax.broadcasted_iota(jnp.int32, picture.shape, 0) + step * tile).astype(jnp.float32)
    row_term = (row - half) * (row - half)
    dist = (row_term + across_ref[...]) / (half * half)
    image = (jnp.exp(rate_ref[...] * dist) * picture).astype(out_ref.dtype)
    for k in range(per_tile):
        out_ref[pl.ds(step * per_tile + k, 1), pl.ds(0, lines), :] = image[
            k * lines:(k + 1) * lines
        ][None]
    widened = image.astype(jnp.float32)
    partial = jnp.sum(widened * widened, axis=0, keepdims=True)

    @pl.when(step == 0)
    def _():
        power_ref[...] = jnp.zeros_like(power_ref)

    power_ref[...] += partial

    @pl.when(step == pl.num_programs(0) - 1)
    def _():
        total = jnp.sum(power_ref[...], axis=1, keepdims=True)
        high = total.astype(out_ref.dtype)
        rest = total - high.astype(jnp.float32)
        middle = rest.astype(out_ref.dtype)
        low = (rest - middle.astype(jnp.float32)).astype(out_ref.dtype)
        lane = lax.broadcasted_iota(jnp.int32, power_ref.shape, 1)
        zero = jnp.zeros(power_ref.shape, out_ref.dtype)
        pieces = jnp.where(
            lane == 0, high, jnp.where(lane == 1, middle, jnp.where(lane == 2, low, zero))
        )
        for f in range(out_ref.shape[0]):
            out_ref[pl.ds(f, 1), pl.ds(lines, 1), :] = pieces[None]


def make_images(table, turned, rate, across, freq_count):
    points, depth = table.shape
    width = turned.shape[1]
    lines = points // freq_count
    tile = 512
    return pl.pallas_call(
        image_kernel,
        grid=(points // tile,),
        in_specs=[
            pl.BlockSpec((tile, depth), lambda i: (i, 0)),
            pl.BlockSpec((depth, width), lambda i: (0, 0)),
            pl.BlockSpec((1, width), lambda i: (0, 0)),
            pl.BlockSpec((1, width), lambda i: (0, 0)),
        ],
        out_specs=pl.BlockSpec((freq_count, lines + 1, width), lambda i: (0, 0, 0)),
        out_shape=jax.ShapeDtypeStruct((freq_count, lines + 1, width), jnp.bfloat16),
        scratch_shapes=[pltpu.VMEM((1, width), jnp.float32)],
        cost_estimate=pl.CostEstimate(
            flops=2 * points * depth * width,
            transcendentals=points * width,
            bytes_accessed=2 * (points * depth + depth * width + points * width),
        ),
    )(table, turned, rate, across)


def body(visibilities, templates):
    channels = visibilities.shape[0]
    row_count = visibilities.shape[2]
    points = visibilities.shape[3]
    num_templates = templates.shape[0]
    freq_count = lax.axis_size("freq")
    sky_count = lax.axis_size("sky")
    all_channels = channels * freq_count
    columns = points // sky_count
    lines = points // freq_count
    cosine, sine, table = tables(points, sky_count, row_count)

    rows = visibilities.reshape(channels * 2 * row_count, points)
    with_cos = jnp.dot(rows, cosine, preferred_element_type=jnp.float32).reshape(
        channels, 2, row_count, points
    )
    with_sin = jnp.dot(rows, sine, preferred_element_type=jnp.float32).reshape(
        channels, 2, row_count, points
    )
    send = make_send(with_cos, with_sin, sky_count, columns)
    turned = lax.all_to_all(send, "sky", 0, 0, tiled=True)
    turned = turned.reshape(sky_count * 2 * row_count, channels * columns)

    col_pos = (lax.axis_index("sky") * columns + jnp.arange(columns, dtype=jnp.int32)).astype(
        jnp.float32
    )
    chan_pos = (lax.axis_index("freq") * channels + jnp.arange(channels, dtype=jnp.int32)).astype(
        jnp.float32
    )
    stretch = 1.0 + 0.5 * chan_pos / jnp.float32(all_channels - 1)
    coef = -0.7 * stretch * stretch
    half = jnp.float32(points / 2.0)
    rate = jnp.broadcast_to(coef[:, None], (channels, columns)).reshape(1, channels * columns)
    across = jnp.broadcast_to(
        ((col_pos - half) * (col_pos - half))[None, :], (channels, columns)
    ).reshape(1, channels * columns)
    outgoing = make_images(table, turned, rate, across, freq_count)
    gathered = lax.all_to_all(outgoing, "freq", 0, 0, tiled=True)
    power_freq = jnp.sum(gathered[:, lines, :3].astype(jnp.float32))
    column_power = lax.all_to_all(
        jnp.broadcast_to(power_freq, (sky_count, 128)), "sky", 0, 0, tiled=True
    )
    power_sum = jnp.sum(column_power[:, 0])
    images = gathered[:, :lines].reshape(freq_count, lines, channels, columns)
    weights = filters(templates, all_channels, ORDER).reshape(-1, freq_count, channels)
    result = jnp.einsum(
        "kfc,flcm->klm", weights, images, preferred_element_type=jnp.float32
    )
    spread = jnp.sqrt(power_sum / (all_channels * points * points) + epsilon)
    return (result[:num_templates] / spread, result[num_templates:])


def solution(mesh):
    return jax.shard_map(
        body,
        mesh=mesh,
        in_specs=(P("freq", None, "sky", None), P()),
        out_specs=(P(None, "freq", "sky"), P(None, "freq", "sky")),
        check_vma=False,
    )
```
